256 devices in a mesh: row: 16 (over z_lo, x, core), col: 16 (over z_hi, y).
Axes of the slice: x: 4, y: 4, z: 8 (z_hi: 4, z_lo: 2; z = z_hi * 2 + z_lo), core: 2. Of those that a mesh axis runs over, the one named last changes fastest.
Arguments:
- features: bfloat16 [65536, 512], P(('col', 'row')), may hold values from -6 to 6
- weight: bfloat16 [512, 512], replicated, may hold values from -0.25 to 0.25
- entry_values: bfloat16 [16, 16, 32, 128, 128], P('row', 'col'), may hold values from 0.0009994507 to 0.019897461
- block_rows: int32 [16, 16, 32], P('row', 'col'), may hold values from 0 to 31
- block_cols: int32 [16, 16, 32], P('row', 'col'), may hold values from 0 to 31
- entry_counts: int32 [16, 16], P('row', 'col'), may hold values from 8 to 32, as said below
- cotangent: bfloat16 [65536, 512], P(('row', 'col')), may hold values from -1.5 to 1.5
Outputs:
- output: bfloat16 [65536, 512], P(('row', 'col'))
- grad_features: bfloat16 [65536, 512], P(('col', 'row'))
- grad_weight: float32 [512, 512], replicated
The draws below stay inside these ranges and needn't reach their ends.
Inputs may be any that keep to these rules, and one draw needn't show every extreme that they name: `entry_counts`: each grid cell has at least 8 live slots; at least one cell has all 32 live.
All inputs are finite; a program needn't handle non-finite values.
Results may differ from the reference program's by a relative error of at most 0.022.
Values may be sent and summed in bfloat16 or wider, within the bound.
No kernel may reach another device: no remote copies, remote signals or barrier semaphores. Data moves between devices by JAX's collectives and lax.ppermute only.
A program may use at most 128 MiB of HBM per device.

```python
import math
import jax
import jax.numpy as jnp
from jax import lax

F = 512
BLOCK = 128
ROWS_DEV = 256
ENTRIES = 32
NODES = 65536
ROW_BLOCKS = 32
COL_BLOCKS = 32
N_ROW = 16
N_COL = 16


def draw_entry_counts(key, part):
    keys = jax.random.split(jax.random.fold_in(key, 7), 3)
    lowest = ENTRIES // 4
    first = jax.random.randint(keys[0], (N_ROW * N_COL,), lowest, ENTRIES + 1)
    second = jax.random.randint(keys[1], (N_ROW * N_COL,), lowest, ENTRIES + 1)
    chosen = jax.random.randint(keys[2], (), 0, N_ROW * N_COL)
    counts = jnp.where(jnp.arange(N_ROW * N_COL) == chosen, ENTRIES, jnp.minimum(first, second))
    return counts.reshape(N_ROW, N_COL).astype(jnp.int32)


def with_ends(values, rng, least, high):
    extent = values.shape
    spot = [jax.random.randint(jax.random.fold_in(rng, axis), (), 0, extent[axis]) for axis in range(len(extent))]
    values = values.at[tuple(spot)].set(least)
    longest = extent.index(max(extent))
    spot[longest] = (spot[longest] + 1) % extent[longest]
    return values.at[tuple(spot)].set(high)


def level_of(own_key, dims, cuts, smallest, high):
    factor_of = 1.0
    for dim, parts in cuts:
        draws = jax.random.uniform(jax.random.fold_in(jax.random.fold_in(own_key, 6), dim), (parts,), jnp.float32, smallest / len(cuts), high / len(cuts))
        factor_of = factor_of * jnp.repeat(jnp.exp(draws), dims[dim] // parts).reshape((-1,) + (1,) * (len(dims) - 1 - dim))
    return factor_of


def centred(key, shape, deviation, limit, shards=(), kind=jnp.bfloat16):
    array = jax.random.normal(key, shape, jnp.float32) * deviation
    if len(shards) > 0:
        array = level_of(key, shape, shards, -0.22, 0.18) * array
    return jnp.clip(array, min=-limit, max=limit).astype(kind)


def setup_inputs(seed: int = 0) -> dict:
    key_of = jax.random.split(jax.random.key(seed), 8)
    features = centred(key_of[0], (NODES, F), 1.0, 6.0, ((0, 256),))
    weight = centred(key_of[1], (F, F), F ** -0.5, 0.25)
    entry_values = jnp.clip(jnp.exp(math.log(0.019897461) - 2.9911416 * jax.random.uniform(key_of[2], (N_ROW, N_COL, ENTRIES, BLOCK, BLOCK), jnp.float32) ** level_of(key_of[2], (N_ROW, N_COL, ENTRIES, BLOCK, BLOCK), ((0, 16), (1, 16)), -0.2, 0.2)), 0.0009994507, 0.019897461).astype(jnp.bfloat16)
    block_rows = with_ends(jax.random.randint(key_of[3], (N_ROW, N_COL, ENTRIES), 0, ROW_BLOCKS), jax.random.fold_in(key_of[3], 1), 0, ROW_BLOCKS - 1).astype(jnp.int32)
    block_cols = with_ends(jax.random.randint(key_of[4], (N_ROW, N_COL, ENTRIES), 0, COL_BLOCKS), jax.random.fold_in(key_of[4], 1), 0, COL_BLOCKS - 1).astype(jnp.int32)
    entry_counts = draw_entry_counts(jax.random.fold_in(key_of[7], 71), 0)
    cotangent = centred(key_of[6], (NODES, F), 0.25, 1.5, ((0, 256),))
    return {"features": features, "weight": weight, "entry_values": entry_values, "block_rows": block_rows, "block_cols": block_cols, "entry_counts": entry_counts, "cotangent": cotangent}


def cell_sum(values, source_ids, target_ids, live_count, source, target_blocks, transpose):
    feature_count = source.shape[1]
    tiles = source.reshape(-1, BLOCK, feature_count)[source_ids].astype(jnp.float32)
    matrices = values.astype(jnp.float32)
    if transpose:
        products = jnp.einsum("kba,kbf->kaf", matrices, tiles)
    else:
        products = jnp.einsum("kab,kbf->kaf", matrices, tiles)
    alive_mask = (jnp.arange(ENTRIES) < live_count).astype(jnp.float32)
    selector = (target_ids[None, :] == jnp.arange(target_blocks)[:, None]).astype(jnp.float32) * alive_mask[None, :]
    running = jnp.einsum("rk,kaf->raf", selector, products, precision=lax.Precision.HIGHEST)
    return running.reshape(target_blocks * BLOCK, feature_count)


def rounded(value):
    return lax.optimization_barrier(value.astype(jnp.bfloat16)).astype(jnp.float32)


def reference(features, weight, entry_values, block_rows, block_cols, entry_counts, cotangent):
    projected = jnp.dot(features, weight, preferred_element_type=jnp.float32).astype(jnp.bfloat16)
    row_span = N_COL * ROWS_DEV
    col_span = N_ROW * ROWS_DEV

    def forward_row(i):
        def over_cols(j, running):
            start = (j * col_span).astype(jnp.int32)
            panel = lax.dynamic_slice_in_dim(projected, start, col_span, 0)
            term = cell_sum(entry_values[i, j], block_cols[i, j], block_rows[i, j], entry_counts[i, j], panel, ROW_BLOCKS, False)
            return running + rounded(term)
        return lax.fori_loop(0, N_COL, over_cols, jnp.zeros((row_span, F), jnp.float32))

    pre = lax.map(forward_row, jnp.arange(N_ROW, dtype=jnp.int32)).reshape(NODES, F)
    output = jax.nn.silu(pre).astype(jnp.bfloat16)
    sigmoid_value = jax.nn.sigmoid(pre)
    upstream = (cotangent.astype(jnp.float32) * sigmoid_value * (1.0 + pre * (1.0 - sigmoid_value))).astype(jnp.bfloat16)

    def backward_col(j):
        def over_rows(i, running):
            start = (i * row_span).astype(jnp.int32)
            panel = lax.dynamic_slice_in_dim(upstream, start, row_span, 0)
            term = cell_sum(entry_values[i, j], block_rows[i, j], block_cols[i, j], entry_counts[i, j], panel, COL_BLOCKS, True)
            return running + rounded(term)
        return lax.fori_loop(0, N_ROW, over_rows, jnp.zeros((col_span, F), jnp.float32))

    grad_projected = lax.map(backward_col, jnp.arange(N_COL, dtype=jnp.int32)).reshape(NODES, F).astype(jnp.bfloat16)
    grad_weight = jnp.dot(features.T, grad_projected, preferred_element_type=jnp.float32)
    grad_features = jnp.dot(grad_projected, weight.T, preferred_element_type=jnp.float32).astype(jnp.bfloat16)
    return (output, grad_features, grad_weight)
```

```python
import jax
import jax.numpy as jnp
from jax import lax
from jax.sharding import PartitionSpec as P


def block_terms(values, source_ids, target_ids, live_count, source, target_blocks, transpose):
    entry_total = values.shape[0]
    block_side = values.shape[1]
    feature_count = source.shape[1]
    group_size = min(32, entry_total)
    source_tiles = source.reshape(-1, block_side, feature_count)

    def one_group(group_index, running):
        first_entry = group_index * group_size
        tiles = jnp.take(source_tiles, source_ids, axis=0)
        if transpose:
            products = jnp.einsum("kba,kbf->kaf", values, tiles, preferred_element_type=jnp.float32)
        else:
            products = jnp.einsum("kab,kbf->kaf", values, tiles, preferred_element_type=jnp.float32)
        alive_mask = (first_entry + jnp.arange(group_size) < live_count).astype(jnp.float32)
        return running.at[target_ids].add(products * alive_mask[:, None, None])

    zero_sum = jnp.zeros((target_blocks, block_side, feature_count), jnp.float32)
    trip_count = entry_total // group_size
    running = lax.fori_loop(0, trip_count, one_group, zero_sum)
    return running.reshape(target_blocks * block_side, feature_count)


def silu_slope(summed):
    sigmoid_value = jax.nn.sigmoid(summed)
    return sigmoid_value * (1.0 + summed * (1.0 - sigmoid_value))


def shards(features, weight, entry_values, block_rows, block_cols, entry_counts, cotangent):
    values = entry_values[0, 0]
    row_ids = block_rows[0, 0]
    col_ids = block_cols[0, 0]
    live_count = entry_counts[0, 0]
    local_rows = features.shape[0]
    block_side = values.shape[1]
    row_span = lax.axis_size("col") * local_rows
    col_span = lax.axis_size("row") * local_rows
    projected = jnp.dot(features, weight, preferred_element_type=jnp.float32).astype(jnp.bfloat16)
    panel = lax.all_gather(projected, "row", axis=0, tiled=True)
    forward_terms = block_terms(
        values, col_ids, row_ids, live_count, panel, row_span // block_side, False
    )
    own_sum = lax.psum_scatter(
        forward_terms.astype(jnp.bfloat16), "col", scatter_dimension=0, tiled=True
    ).astype(jnp.float32)
    output = jax.nn.silu(own_sum).astype(jnp.bfloat16)
    own_upstream = (cotangent.astype(jnp.float32) * silu_slope(own_sum)).astype(jnp.bfloat16)
    upstream = lax.all_gather(own_upstream, "col", axis=0, tiled=True)
    backward_terms = block_terms(
        values, row_ids, col_ids, live_count, upstream, col_span // block_side, True
    )
    grad_projected = lax.psum_scatter(
        backward_terms.astype(jnp.bfloat16), "row", scatter_dimension=0, tiled=True
    )
    weight_term = lax.dot_general(
        features, grad_projected, (((0,), (0,)), ((), ())), preferred_element_type=jnp.float32
    )
    weight_part = lax.psum_scatter(weight_term, "row", scatter_dimension=0, tiled=True)
    weight_part = lax.psum(weight_part, "col")
    grad_weight = lax.all_gather(weight_part, "row", axis=0, tiled=True)
    grad_features = lax.dot_general(
        grad_projected, weight, (((1,), (1,)), ((), ())), preferred_element_type=jnp.float32
    ).astype(jnp.bfloat16)
    return (output, grad_features, grad_weight)


def solution(mesh):
    placed = (
        P(("col", "row"), None),
        P(),
        P("row", "col", None, None, None),
        P("row", "col", None),
        P("row", "col", None),
        P("row", "col"),
        P(("row", "col"), None),
    )
    return jax.shard_map(
        shards,
        mesh=mesh,
        in_specs=placed,
        out_specs=(P(("row", "col"), None), P(("col", "row"), None), P()),
        check_vma=False,
    )
```

```python
import jax
import jax.numpy as jnp
from jax import lax
from jax.sharding import PartitionSpec as P


def block_terms(values, source_ids, target_ids, live_count, source, target_blocks, transpose):
    entry_total = values.shape[0]
    block_side = values.shape[1]
    feature_count = source.shape[1]
    group_size = min(32, entry_total)
    source_tiles = source.reshape(-1, block_side, feature_count)

    def one_group(group_index, running):
        first_entry = group_index * group_size
        tiles = jnp.take(source_tiles, source_ids, axis=0)
        if transpose:
            products = jnp.einsum("kba,kbf->kaf", values, tiles, preferred_element_type=jnp.float32)
        else:
            products = jnp.einsum("kab,kbf->kaf", values, tiles, preferred_element_type=jnp.float32)
        alive_mask = (first_entry + jnp.arange(group_size) < live_count).astype(jnp.float32)
        return running.at[target_ids].add(products * alive_mask[:, None, None])

    zero_sum = jnp.zeros((target_blocks, block_side, feature_count), jnp.float32)
    trip_count = entry_total // group_size
    running = lax.fori_loop(0, trip_count, one_group, zero_sum)
    return running.reshape(target_blocks * block_side, feature_count)


def exchange_sum(parts, axis_name):
    count = lax.axis_size(axis_name)
    pieces = parts.reshape((count, -1) + parts.shape[1:])
    pieces = lax.all_to_all(pieces, axis_name, 0, 0, tiled=False)
    return pieces.astype(jnp.float32).sum(0)


def exchange_gather(part, axis_name):
    count = lax.axis_size(axis_name)
    pieces = jnp.broadcast_to(part[None], (count,) + part.shape)
    pieces = lax.all_to_all(pieces, axis_name, 0, 0, tiled=False)
    return pieces.reshape((-1,) + part.shape[1:])


def silu_slope(summed):
    sigmoid_value = jax.nn.sigmoid(summed)
    return sigmoid_value * (1.0 + summed * (1.0 - sigmoid_value))


def shards(features, weight, entry_values, block_rows, block_cols, entry_counts, cotangent):
    values = entry_values[0, 0]
    row_ids = block_rows[0, 0]
    col_ids = block_cols[0, 0]
    live_count = entry_counts[0, 0]
    local_rows = features.shape[0]
    block_side = values.shape[1]
    row_span = lax.axis_size("col") * local_rows
    col_span = lax.axis_size("row") * local_rows
    projected = jnp.dot(features, weight, preferred_element_type=jnp.float32).astype(jnp.bfloat16)
    panel = lax.all_gather(projected, "row", axis=0, tiled=True)
    forward_terms = block_terms(
        values, col_ids, row_ids, live_count, panel, row_span // block_side, False
    )
    own_sum = exchange_sum(forward_terms.astype(jnp.bfloat16), "col")
    output = jax.nn.silu(own_sum).astype(jnp.bfloat16)
    own_upstream = (cotangent.astype(jnp.float32) * silu_slope(own_sum)).astype(jnp.bfloat16)
    upstream = lax.all_gather(own_upstream, "col", axis=0, tiled=True)
    backward_terms = block_terms(
        values, row_ids, col_ids, live_count, upstream, col_span // block_side, True
    )
    grad_projected = exchange_sum(backward_terms.astype(jnp.bfloat16), "row").astype(jnp.bfloat16)
    weight_term = lax.dot_general(
        features, grad_projected, (((0,), (0,)), ((), ())), preferred_element_type=jnp.float32
    )
    weight_part = exchange_sum(exchange_sum(weight_term, "row"), "col")
    grad_weight = exchange_gather(exchange_gather(weight_part, "col"), "row")
    grad_features = lax.dot_general(
        grad_projected, weight, (((1,), (1,)), ((), ())), preferred_element_type=jnp.float32
    ).astype(jnp.bfloat16)
    return (output, grad_features, grad_weight)


def solution(mesh):
    placed = (
        P(("col", "row"), None),
        P(),
        P("row", "col", None, None, None),
        P("row", "col", None),
        P("row", "col", None),
        P("row", "col"),
        P(("row", "col"), None),
    )
    return jax.shard_map(
        shards,
        mesh=mesh,
        in_specs=placed,
        out_specs=(P(("row", "col"), None), P(("col", "row"), None), P()),
        check_vma=False,
    )
```

```python
import functools
import jax
import jax.numpy as jnp
from jax import lax
from jax.experimental import pallas as pl
from jax.experimental.pallas import tpu as pltpu
from jax.sharding import PartitionSpec as P


def block_kernel(source_ids, target_ids, live, values_ref, tile_ref, out_ref, acc_ref, *, transpose):
    k = pl.program_id(0)

    @pl.when(k == 0)
    def _():
        acc_ref[...] = jnp.zeros_like(acc_ref)

    @pl.when(k < live[0])
    def _():
        block = values_ref[...]
        if transpose:
            term = lax.dot_general(block, tile_ref[...], (((0,), (0,)), ((), ())), preferred_element_type=jnp.float32)
        else:
            term = jnp.dot(block, tile_ref[...], preferred_element_type=jnp.float32)
        target = target_ids[k]
        acc_ref[target] += term

    @pl.when(k == pl.num_programs(0) - 1)
    def _():
        out_ref[...] = acc_ref[...].reshape(out_ref.shape).astype(out_ref.dtype)


def block_terms(values, source_ids, target_ids, live_count, source, target_blocks, transpose):
    entry_total, block_side, _ = values.shape
    feature_count = source.shape[1]
    live = jnp.reshape(live_count, (1,)).astype(jnp.int32)

    def entry_of(k, live):
        return jnp.minimum(k, live[0] - 1)

    def values_map(k, source_ids, target_ids, live):
        return (entry_of(k, live), 0, 0)

    def tile_map(k, source_ids, target_ids, live):
        return (source_ids[entry_of(k, live)], 0)

    def out_map(k, source_ids, target_ids, live):
        return (0, 0)

    grid_spec = pltpu.PrefetchScalarGridSpec(
        num_scalar_prefetch=3,
        grid=(entry_total,),
        in_specs=[
            pl.BlockSpec((None, block_side, block_side), values_map),
            pl.BlockSpec((block_side, feature_count), tile_map),
        ],
        out_specs=pl.BlockSpec((target_blocks * block_side, feature_count), out_map),
        scratch_shapes=[pltpu.VMEM((target_blocks, block_side, feature_count), jnp.float32)],
    )
    return pl.pallas_call(
        functools.partial(block_kernel, transpose=transpose),
        grid_spec=grid_spec,
        out_shape=jax.ShapeDtypeStruct((target_blocks * block_side, feature_count), jnp.bfloat16),
        compiler_params=pltpu.CompilerParams(dimension_semantics=("arbitrary",)),
    )(source_ids, target_ids, live, values, source)


def exchange_sum(parts, axis_name):
    count = lax.axis_size(axis_name)
    pieces = parts.reshape((count, -1) + parts.shape[1:])
    pieces = lax.all_to_all(pieces, axis_name, 0, 0, tiled=False)
    return pieces.astype(jnp.float32).sum(0)


def exchange_gather(part, axis_name):
    count = lax.axis_size(axis_name)
    pieces = jnp.broadcast_to(part[None], (count,) + part.shape)
    pieces = lax.all_to_all(pieces, axis_name, 0, 0, tiled=False)
    return pieces.reshape((-1,) + part.shape[1:])


def silu_slope(summed):
    sigmoid_value = jax.nn.sigmoid(summed)
    return sigmoid_value * (1.0 + summed * (1.0 - sigmoid_value))


def shards(features, weight, entry_values, block_rows, block_cols, entry_counts, cotangent):
    values = entry_values[0, 0]
    row_ids = block_rows[0, 0]
    col_ids = block_cols[0, 0]
    live_count = entry_counts[0, 0]
    local_rows = features.shape[0]
    block_side = values.shape[1]
    row_span = lax.axis_size("col") * local_rows
    col_span = lax.axis_size("row") * local_rows
    projected = jnp.dot(features, weight, preferred_element_type=jnp.float32).astype(jnp.bfloat16)
    panel = lax.all_gather(projected, "row", axis=0, tiled=True)
    forward_terms = block_terms(
        values, col_ids, row_ids, live_count, panel, row_span // block_side, False
    )
    own_sum = exchange_sum(forward_terms.astype(jnp.bfloat16), "col")
    output = jax.nn.silu(own_sum).astype(jnp.bfloat16)
    own_upstream = (cotangent.astype(jnp.float32) * silu_slope(own_sum)).astype(jnp.bfloat16)
    upstream = lax.all_gather(own_upstream, "col", axis=0, tiled=True)
    backward_terms = block_terms(
        values, row_ids, col_ids, live_count, upstream, col_span // block_side, True
    )
    grad_projected = exchange_sum(backward_terms.astype(jnp.bfloat16), "row").astype(jnp.bfloat16)
    weight_term = lax.dot_general(
        features, grad_projected, (((0,), (0,)), ((), ())), preferred_element_type=jnp.float32
    )
    weight_part = exchange_sum(exchange_sum(weight_term, "row"), "col")
    grad_weight = exchange_gather(exchange_gather(weight_part, "col"), "row")
    grad_features = lax.dot_general(
        grad_projected, weight, (((1,), (1,)), ((), ())), preferred_element_type=jnp.float32
    ).astype(jnp.bfloat16)
    return (output, grad_features, grad_weight)


def solution(mesh):
    placed = (
        P(("col", "row"), None),
        P(),
        P("row", "col", None, None, None),
        P("row", "col", None),
        P("row", "col", None),
        P("row", "col"),
        P(("row", "col"), None),
    )
    return jax.shard_map(
        shards,
        mesh=mesh,
        in_specs=placed,
        out_specs=(P(("row", "col"), None), P(("col", "row"), None), P()),
        check_vma=False,
    )
```

```python
import functools
import jax
import jax.numpy as jnp
from jax import lax
from jax.experimental import pallas as pl
from jax.experimental.pallas import tpu as pltpu
from jax.sharding import PartitionSpec as P

CHUNKS = 2


def block_kernel(source_ids, target_ids, live, values_ref, tile_ref, out_ref, acc_ref, *, transpose):
    k = pl.program_id(0)

    @pl.when(k == 0)
    def _():
        acc_ref[...] = jnp.zeros_like(acc_ref)

    @pl.when(k < live[0])
    def _():
        block = values_ref[...]
        if transpose:
            term = lax.dot_general(block, tile_ref[...], (((0,), (0,)), ((), ())), preferred_element_type=jnp.float32)
        else:
            term = jnp.dot(block, tile_ref[...], preferred_element_type=jnp.float32)
        target = target_ids[k]
        acc_ref[target] += term

    @pl.when(k == pl.num_programs(0) - 1)
    def _():
        out_ref[...] = acc_ref[...].reshape(out_ref.shape).astype(out_ref.dtype)


def block_terms(values, source_ids, target_ids, live_count, source, target_blocks, transpose):
    entry_total, block_side, _ = values.shape
    feature_count = source.shape[1]
    live = jnp.reshape(live_count, (1,)).astype(jnp.int32)

    def entry_of(k, live):
        return jnp.minimum(k, live[0] - 1)

    def values_map(k, source_ids, target_ids, live):
        return (entry_of(k, live), 0, 0)

    def tile_map(k, source_ids, target_ids, live):
        return (source_ids[entry_of(k, live)], 0)

    def out_map(k, source_ids, target_ids, live):
        return (0, 0)

    grid_spec = pltpu.PrefetchScalarGridSpec(
        num_scalar_prefetch=3,
        grid=(entry_total,),
        in_specs=[
            pl.BlockSpec((None, block_side, block_side), values_map),
            pl.BlockSpec((block_side, feature_count), tile_map),
        ],
        out_specs=pl.BlockSpec((target_blocks * block_side, feature_count), out_map),
        scratch_shapes=[pltpu.VMEM((target_blocks, block_side, feature_count), jnp.float32)],
    )
    return pl.pallas_call(
        functools.partial(block_kernel, transpose=transpose),
        grid_spec=grid_spec,
        out_shape=jax.ShapeDtypeStruct((target_blocks * block_side, feature_count), jnp.bfloat16),
        compiler_params=pltpu.CompilerParams(dimension_semantics=("arbitrary",)),
    )(source_ids, target_ids, live, values, source)


def exchange_sum(parts, axis_name):
    count = lax.axis_size(axis_name)
    pieces = parts.reshape((count, -1) + parts.shape[1:])
    pieces = lax.all_to_all(pieces, axis_name, 0, 0, tiled=False)
    return pieces.astype(jnp.float32).sum(0)


def exchange_gather(part, axis_name):
    count = lax.axis_size(axis_name)
    pieces = jnp.broadcast_to(part[None], (count,) + part.shape)
    pieces = lax.all_to_all(pieces, axis_name, 0, 0, tiled=False)
    return pieces.reshape((-1,) + part.shape[1:])


def silu_slope(summed):
    sigmoid_value = jax.nn.sigmoid(summed)
    return sigmoid_value * (1.0 + summed * (1.0 - sigmoid_value))


def shards(features, weight, entry_values, block_rows, block_cols, entry_counts, cotangent):
    values = entry_values[0, 0]
    row_ids = block_rows[0, 0]
    col_ids = block_cols[0, 0]
    live_count = entry_counts[0, 0]
    local_rows = features.shape[0]
    block_side = values.shape[1]
    row_span = lax.axis_size("col") * local_rows
    col_span = lax.axis_size("row") * local_rows
    width = weight.shape[1] // CHUNKS
    outputs, weight_terms, feature_terms = [], [], []
    for part in range(CHUNKS):
        weight_cols = weight[:, part * width:(part + 1) * width]
        projected = jnp.dot(features, weight_cols, preferred_element_type=jnp.float32).astype(jnp.bfloat16)
        panel = lax.all_gather(projected, "row", axis=0, tiled=True)
        forward_terms = block_terms(
            values, col_ids, row_ids, live_count, panel, row_span // block_side, False
        )
        own_sum = exchange_sum(forward_terms, "col")
        outputs.append(jax.nn.silu(own_sum).astype(jnp.bfloat16))
        own_cotangent = cotangent[:, part * width:(part + 1) * width].astype(jnp.float32)
        own_upstream = (own_cotangent * silu_slope(own_sum)).astype(jnp.bfloat16)
        upstream = lax.all_gather(own_upstream, "col", axis=0, tiled=True)
        backward_terms = block_terms(
            values, row_ids, col_ids, live_count, upstream, col_span // block_side, True
        )
        grad_projected = exchange_sum(backward_terms, "row").astype(jnp.bfloat16)
        weight_terms.append(lax.dot_general(
            features, grad_projected, (((0,), (0,)), ((), ())), preferred_element_type=jnp.float32
        ))
        feature_terms.append(lax.dot_general(
            grad_projected, weight_cols, (((1,), (1,)), ((), ())), preferred_element_type=jnp.float32
        ))
    output = jnp.concatenate(outputs, axis=1)
    weight_term = jnp.concatenate(weight_terms, axis=1)
    weight_part = exchange_sum(exchange_sum(weight_term, "row"), "col")
    grad_weight = exchange_gather(exchange_gather(weight_part, "col"), "row")
    grad_features = sum(feature_terms).astype(jnp.bfloat16)
    return (output, grad_features, grad_weight)


def solution(mesh):
    placed = (
        P(("col", "row"), None),
        P(),
        P("row", "col", None, None, None),
        P("row", "col", None),
        P("row", "col", None),
        P("row", "col"),
        P(("row", "col"), None),
    )
    return jax.shard_map(
        shards,
        mesh=mesh,
        in_specs=placed,
        out_specs=(P(("row", "col"), None), P(("col", "row"), None), P()),
        check_vma=False,
    )
```

```python
import functools
import jax
import jax.numpy as jnp
from jax import lax
from jax.experimental import pallas as pl
from jax.experimental.pallas import tpu as pltpu
from jax.sharding import PartitionSpec as P


def block_kernel(source_ids, target_ids, live, values_ref, tile_ref, out_ref, acc_ref, *, transpose):
    k = pl.program_id(0)

    @pl.when(k == 0)
    def _():
        acc_ref[...] = jnp.zeros_like(acc_ref)

    @pl.when(k < live[0])
    def _():
        block = values_ref[...]
        if transpose:
            term = lax.dot_general(block, tile_ref[...], (((0,), (0,)), ((), ())), preferred_element_type=jnp.float32)
        else:
            term = jnp.dot(block, tile_ref[...], preferred_element_type=jnp.float32)
        target = target_ids[k]
        acc_ref[target] += term

    @pl.when(k == pl.num_programs(0) - 1)
    def _():
        out_ref[...] = acc_ref[...].reshape(out_ref.shape).astype(out_ref.dtype)


def block_terms(values, source_ids, target_ids, live_count, source, target_blocks, transpose):
    entry_total, block_side, _ = values.shape
    feature_count = source.shape[1]
    live = jnp.reshape(live_count, (1,)).astype(jnp.int32)

    def entry_of(k, live):
        return jnp.minimum(k, live[0] - 1)

    def values_map(k, source_ids, target_ids, live):
        return (entry_of(k, live), 0, 0)

    def tile_map(k, source_ids, target_ids, live):
        return (source_ids[entry_of(k, live)], 0)

    def out_map(k, source_ids, target_ids, live):
        return (0, 0)

    grid_spec = pltpu.PrefetchScalarGridSpec(
        num_scalar_prefetch=3,
        grid=(entry_total,),
        in_specs=[
            pl.BlockSpec((None, block_side, block_side), values_map),
            pl.BlockSpec((block_side, feature_count), tile_map),
        ],
        out_specs=pl.BlockSpec((target_blocks * block_side, feature_count), out_map),
        scratch_shapes=[pltpu.VMEM((target_blocks, block_side, feature_count), jnp.float32)],
    )
    return pl.pallas_call(
        functools.partial(block_kernel, transpose=transpose),
        grid_spec=grid_spec,
        out_shape=jax.ShapeDtypeStruct((target_blocks * block_side, feature_count), jnp.bfloat16),
        compiler_params=pltpu.CompilerParams(dimension_semantics=("arbitrary",)),
    )(source_ids, target_ids, live, values, source)


def exchange_sum(parts, axis_name):
    count = lax.axis_size(axis_name)
    pieces = parts.reshape((count, -1) + parts.shape[1:])
    pieces = lax.all_to_all(pieces, axis_name, 0, 0, tiled=False)
    return pieces.astype(jnp.float32).sum(0)


def exchange_gather(part, axis_name):
    count = lax.axis_size(axis_name)
    pieces = jnp.broadcast_to(part[None], (count,) + part.shape)
    pieces = lax.all_to_all(pieces, axis_name, 0, 0, tiled=False)
    return pieces.reshape((-1,) + part.shape[1:])


def silu_slope(summed):
    sigmoid_value = jax.nn.sigmoid(summed)
    return sigmoid_value * (1.0 + summed * (1.0 - sigmoid_value))


def shards(features, weight, entry_values, block_rows, block_cols, entry_counts, cotangent):
    values = entry_values[0, 0]
    row_ids = block_rows[0, 0]
    col_ids = block_cols[0, 0]
    live_count = entry_counts[0, 0]
    local_rows = features.shape[0]
    block_side = values.shape[1]
    row_span = lax.axis_size("col") * local_rows
    col_span = lax.axis_size("row") * local_rows
    panel = lax.all_gather(features, "row", axis=0, tiled=True)
    forward_terms = block_terms(
        values, col_ids, row_ids, live_count, panel, row_span // block_side, False
    )
    own_mixed = exchange_sum(forward_terms, "col").astype(jnp.bfloat16)
    own_sum = jnp.dot(own_mixed, weight, preferred_element_type=jnp.float32)
    output = jax.nn.silu(own_sum).astype(jnp.bfloat16)
    own_upstream = (cotangent.astype(jnp.float32) * silu_slope(own_sum)).astype(jnp.bfloat16)
    weight_term = lax.dot_general(
        own_mixed, own_upstream, (((0,), (0,)), ((), ())), preferred_element_type=jnp.float32
    )
    weight_part = exchange_sum(exchange_sum(weight_term, "row"), "col")
    grad_weight = exchange_gather(exchange_gather(weight_part, "col"), "row")
    upstream = lax.all_gather(own_upstream, "col", axis=0, tiled=True)
    backward_terms = block_terms(
        values, row_ids, col_ids, live_count, upstream, col_span // block_side, True
    )
    grad_projected = exchange_sum(backward_terms, "row").astype(jnp.bfloat16)
    grad_features = lax.dot_general(
        grad_projected, weight, (((1,), (1,)), ((), ())), preferred_element_type=jnp.float32
    ).astype(jnp.bfloat16)
    return (output, grad_features, grad_weight)


def solution(mesh):
    placed = (
        P(("col", "row"), None),
        P(),
        P("row", "col", None, None, None),
        P("row", "col", None),
        P("row", "col", None),
        P("row", "col"),
        P(("row", "col"), None),
    )
    return jax.shard_map(
        shards,
        mesh=mesh,
        in_specs=placed,
        out_specs=(P(("row", "col"), None), P(("col", "row"), None), P()),
        check_vma=False,
    )
```

```python
import functools
import jax
import jax.numpy as jnp
from jax import lax
from jax.experimental import pallas as pl
from jax.experimental.pallas import tpu as pltpu
from jax.sharding import PartitionSpec as P

GROUP = 4


def block_kernel(source_ids, target_ids, live, values_ref, *refs, transpose):
    tile_refs, out_ref, acc_ref = refs[:-2], refs[-2], refs[-1]
    step = pl.program_id(0)
    group = len(tile_refs)

    @pl.when(step == 0)
    def _():
        acc_ref[...] = jnp.zeros_like(acc_ref)

    for slot, tile_ref in enumerate(tile_refs):
        entry = step * group + slot

        @pl.when(entry < live[0])
        def _():
            block = values_ref[slot]
            if transpose:
                term = lax.dot_general(block, tile_ref[...], (((0,), (0,)), ((), ())), preferred_element_type=jnp.float32)
            else:
                term = jnp.dot(block, tile_ref[...], preferred_element_type=jnp.float32)
            acc_ref[target_ids[entry]] += term

    @pl.when(step == pl.num_programs(0) - 1)
    def _():
        out_ref[...] = acc_ref[...].reshape(out_ref.shape).astype(out_ref.dtype)


def block_terms(values, source_ids, target_ids, live_count, source, target_blocks, transpose):
    entry_total, block_side, _ = values.shape
    feature_count = source.shape[1]
    group = GROUP
    live = jnp.reshape(live_count, (1,)).astype(jnp.int32)

    def values_map(step, source_ids, target_ids, live):
        return (jnp.minimum(step, (live[0] - 1) // group), 0, 0)

    def tile_map_of(slot):
        def tile_map(step, source_ids, target_ids, live):
            return (source_ids[jnp.minimum(step * group + slot, live[0] - 1)], 0)
        return tile_map

    def out_map(step, source_ids, target_ids, live):
        return (0, 0)

    grid_spec = pltpu.PrefetchScalarGridSpec(
        num_scalar_prefetch=3,
        grid=(entry_total // group,),
        in_specs=[pl.BlockSpec((group, block_side, block_side), values_map)]
        + [pl.BlockSpec((block_side, feature_count), tile_map_of(slot)) for slot in range(group)],
        out_specs=pl.BlockSpec((target_blocks * block_side, feature_count), out_map),
        scratch_shapes=[pltpu.VMEM((target_blocks, block_side, feature_count), jnp.float32)],
    )
    return pl.pallas_call(
        functools.partial(block_kernel, transpose=transpose),
        grid_spec=grid_spec,
        out_shape=jax.ShapeDtypeStruct((target_blocks * block_side, feature_count), jnp.bfloat16),
        compiler_params=pltpu.CompilerParams(dimension_semantics=("arbitrary",)),
    )(source_ids, target_ids, live, values, *([source] * group))


def exchange_sum(parts, axis_name):
    count = lax.axis_size(axis_name)
    pieces = parts.reshape((count, -1) + parts.shape[1:])
    pieces = lax.all_to_all(pieces, axis_name, 0, 0, tiled=False)
    return pieces.astype(jnp.float32).sum(0)


def exchange_gather(part, axis_name):
    count = lax.axis_size(axis_name)
    pieces = jnp.broadcast_to(part[None], (count,) + part.shape)
    pieces = lax.all_to_all(pieces, axis_name, 0, 0, tiled=False)
    return pieces.reshape((-1,) + part.shape[1:])


def silu_slope(summed):
    sigmoid_value = jax.nn.sigmoid(summed)
    return sigmoid_value * (1.0 + summed * (1.0 - sigmoid_value))


def shards(features, weight, entry_values, block_rows, block_cols, entry_counts, cotangent):
    values = entry_values[0, 0]
    row_ids = block_rows[0, 0]
    col_ids = block_cols[0, 0]
    live_count = entry_counts[0, 0]
    local_rows = features.shape[0]
    block_side = values.shape[1]
    row_span = lax.axis_size("col") * local_rows
    col_span = lax.axis_size("row") * local_rows
    panel = lax.all_gather(features, "row", axis=0, tiled=True)
    forward_terms = block_terms(
        values, col_ids, row_ids, live_count, panel, row_span // block_side, False
    )
    own_mixed = exchange_sum(forward_terms, "col").astype(jnp.bfloat16)
    own_sum = jnp.dot(own_mixed, weight, preferred_element_type=jnp.float32)
    output = jax.nn.silu(own_sum).astype(jnp.bfloat16)
    own_upstream = (cotangent.astype(jnp.float32) * silu_slope(own_sum)).astype(jnp.bfloat16)
    weight_term = lax.dot_general(
        own_mixed, own_upstream, (((0,), (0,)), ((), ())), preferred_element_type=jnp.float32
    )
    weight_part = exchange_sum(exchange_sum(weight_term, "row"), "col")
    grad_weight = exchange_gather(exchange_gather(weight_part, "col"), "row")
    upstream = lax.all_gather(own_upstream, "col", axis=0, tiled=True)
    backward_terms = block_terms(
        values, row_ids, col_ids, live_count, upstream, col_span // block_side, True
    )
    grad_projected = exchange_sum(backward_terms, "row").astype(jnp.bfloat16)
    grad_features = lax.dot_general(
        grad_projected, weight, (((1,), (1,)), ((), ())), preferred_element_type=jnp.float32
    ).astype(jnp.bfloat16)
    return (output, grad_features, grad_weight)


def solution(mesh):
    placed = (
        P(("col", "row"), None),
        P(),
        P("row", "col", None, None, None),
        P("row", "col", None),
        P("row", "col", None),
        P("row", "col"),
        P(("row", "col"), None),
    )
    return jax.shard_map(
        shards,
        mesh=mesh,
        in_specs=placed,
        out_specs=(P(("row", "col"), None), P(("col", "row"), None), P()),
        check_vma=False,
    )
```

```python
import functools
import jax
import jax.numpy as jnp
from jax import lax
from jax.experimental import pallas as pl
from jax.experimental.pallas import tpu as pltpu
from jax.sharding import Mesh, PartitionSpec as P

GROUP = 4


def block_kernel(source_ids, target_ids, live, values_ref, *refs, transpose):
    tile_refs, out_ref, acc_ref = refs[:-2], refs[-2], refs[-1]
    step = pl.program_id(0)
    group = len(tile_refs)

    @pl.when(step == 0)
    def _():
        acc_ref[...] = jnp.zeros_like(acc_ref)

    for slot, tile_ref in enumerate(tile_refs):
        entry = step * group + slot

        @pl.when(entry < live[0])
        def _():
            block = values_ref[slot]
            if transpose:
                term = lax.dot_general(block, tile_ref[...], (((0,), (0,)), ((), ())), preferred_element_type=jnp.float32)
            else:
                term = jnp.dot(block, tile_ref[...], preferred_element_type=jnp.float32)
            acc_ref[target_ids[entry]] += term

    @pl.when(step == pl.num_programs(0) - 1)
    def _():
        out_ref[...] = acc_ref[...].reshape(out_ref.shape).astype(out_ref.dtype)


def block_terms(values, source_ids, target_ids, live_count, source, target_blocks, transpose):
    entry_total, block_side, _ = values.shape
    feature_count = source.shape[1]
    group = GROUP
    live = jnp.reshape(live_count, (1,)).astype(jnp.int32)

    def values_map(step, source_ids, target_ids, live):
        return (jnp.minimum(step, (live[0] - 1) // group), 0, 0)

    def tile_map_of(slot):
        def tile_map(step, source_ids, target_ids, live):
            return (source_ids[jnp.minimum(step * group + slot, live[0] - 1)], 0)
        return tile_map

    def out_map(step, source_ids, target_ids, live):
        return (0, 0)

    grid_spec = pltpu.PrefetchScalarGridSpec(
        num_scalar_prefetch=3,
        grid=(entry_total // group,),
        in_specs=[pl.BlockSpec((group, block_side, block_side), values_map)]
        + [pl.BlockSpec((block_side, feature_count), tile_map_of(slot)) for slot in range(group)],
        out_specs=pl.BlockSpec((target_blocks * block_side, feature_count), out_map),
        scratch_shapes=[pltpu.VMEM((target_blocks, block_side, feature_count), jnp.float32)],
    )
    return pl.pallas_call(
        functools.partial(block_kernel, transpose=transpose),
        grid_spec=grid_spec,
        out_shape=jax.ShapeDtypeStruct((target_blocks * block_side, feature_count), jnp.bfloat16),
        compiler_params=pltpu.CompilerParams(dimension_semantics=("arbitrary",)),
    )(source_ids, target_ids, live, values, *([source] * group))


ROW = ("zl", "x", "core")
COL = ("zh", "y")


def exchange_sum(parts, axis_name, count):
    pieces = parts.reshape((count, -1) + parts.shape[1:])
    pieces = lax.all_to_all(pieces, axis_name, 0, 0, tiled=False)
    return pieces.astype(jnp.float32).sum(0)


def staged_sum(parts, axes, sizes):
    pieces = parts.reshape(tuple(sizes) + (-1,) + parts.shape[1:])
    for position in reversed(range(len(axes))):
        pieces = lax.all_to_all(pieces, axes[position], position, position, tiled=False)
        pieces = pieces.astype(jnp.float32).sum(position)
        if position > 0:
            pieces = pieces.astype(jnp.bfloat16)
    return pieces


def exchange_gather(part, axis_name, count):
    pieces = jnp.broadcast_to(part[None], (count,) + part.shape)
    pieces = lax.all_to_all(pieces, axis_name, 0, 0, tiled=False)
    return pieces.reshape((-1,) + part.shape[1:])


def silu_slope(summed):
    sigmoid_value = jax.nn.sigmoid(summed)
    return sigmoid_value * (1.0 + summed * (1.0 - sigmoid_value))


def shards(features, weight, entry_values, block_rows, block_cols, entry_counts, cotangent):
    values = entry_values[0, 0]
    row_ids = block_rows[0, 0]
    col_ids = block_cols[0, 0]
    live_count = entry_counts[0, 0]
    local_rows = features.shape[0]
    block_side = values.shape[1]
    row_sizes = [lax.axis_size(name) for name in ROW]
    col_sizes = [lax.axis_size(name) for name in COL]
    row_count = row_sizes[0] * row_sizes[1] * row_sizes[2]
    col_count = col_sizes[0] * col_sizes[1]
    row_span = col_count * local_rows
    col_span = row_count * local_rows
    panel = lax.all_gather(features, ROW, axis=0, tiled=True)
    forward_terms = block_terms(
        values, col_ids, row_ids, live_count, panel, row_span // block_side, False
    )
    own_mixed = staged_sum(forward_terms, COL, col_sizes).astype(jnp.bfloat16)
    own_sum = jnp.dot(own_mixed, weight, preferred_element_type=jnp.float32)
    output = jax.nn.silu(own_sum).astype(jnp.bfloat16)
    own_upstream = (cotangent.astype(jnp.float32) * silu_slope(own_sum)).astype(jnp.bfloat16)
    weight_term = lax.dot_general(
        own_mixed, own_upstream, (((0,), (0,)), ((), ())), preferred_element_type=jnp.float32
    )
    weight_part = exchange_sum(exchange_sum(weight_term, ROW, row_count), COL, col_count)
    grad_weight = exchange_gather(exchange_gather(weight_part, COL, col_count), ROW, row_count)
    upstream = lax.all_gather(own_upstream, COL, axis=0, tiled=True)
    backward_terms = block_terms(
        values, row_ids, col_ids, live_count, upstream, col_span // block_side, True
    )
    grad_projected = staged_sum(backward_terms, ROW, row_sizes).astype(jnp.bfloat16)
    grad_features = lax.dot_general(
        grad_projected, weight, (((1,), (1,)), ((), ())), preferred_element_type=jnp.float32
    ).astype(jnp.bfloat16)
    return (output, grad_features, grad_weight)


def solution(mesh):
    row_parts = (2, 4, 2)
    col_parts = (4, 4)
    split = Mesh(mesh.devices.reshape(row_parts + col_parts), ROW + COL)
    placed = (
        P(COL + ROW, None),
        P(),
        P(ROW, COL, None, None, None),
        P(ROW, COL, None),
        P(ROW, COL, None),
        P(ROW, COL),
        P(ROW + COL, None),
    )
    return jax.shard_map(
        shards,
        mesh=split,
        in_specs=placed,
        out_specs=(P(ROW + COL, None), P(COL + ROW, None), P()),
        check_vma=False,
    )
```

```python
import functools
import jax
import jax.numpy as jnp
from jax import lax
from jax.experimental import pallas as pl
from jax.experimental.pallas import tpu as pltpu
from jax.sharding import Mesh, PartitionSpec as P

GROUP = 4


def block_kernel(source_ids, target_ids, live, values_ref, *refs, transpose):
    tile_refs, out_ref, acc_ref = refs[:-2], refs[-2], refs[-1]
    step = pl.program_id(0)
    group = len(tile_refs)

    @pl.when(step == 0)
    def _():
        acc_ref[...] = jnp.zeros_like(acc_ref)

    for slot, tile_ref in enumerate(tile_refs):
        entry = step * group + slot

        @pl.when(entry < live[0])
        def _():
            block = values_ref[slot]
            if transpose:
                term = lax.dot_general(block, tile_ref[...], (((0,), (0,)), ((), ())), preferred_element_type=jnp.float32)
            else:
                term = jnp.dot(block, tile_ref[...], preferred_element_type=jnp.float32)
            acc_ref[target_ids[entry]] += term

    @pl.when(step == pl.num_programs(0) - 1)
    def _():
        out_ref[...] = acc_ref[...].reshape(out_ref.shape).astype(out_ref.dtype)


def block_terms(values, source_ids, target_ids, live_count, source, target_blocks, transpose):
    entry_total, block_side, _ = values.shape
    feature_count = source.shape[1]
    group = GROUP
    live = jnp.reshape(live_count, (1,)).astype(jnp.int32)

    def values_map(step, source_ids, target_ids, live):
        return (jnp.minimum(step, (live[0] - 1) // group), 0, 0)

    def tile_map_of(slot):
        def tile_map(step, source_ids, target_ids, live):
            return (source_ids[jnp.minimum(step * group + slot, live[0] - 1)], 0)
        return tile_map

    def out_map(step, source_ids, target_ids, live):
        return (0, 0)

    grid_spec = pltpu.PrefetchScalarGridSpec(
        num_scalar_prefetch=3,
        grid=(entry_total // group,),
        in_specs=[pl.BlockSpec((group, block_side, block_side), values_map)]
        + [pl.BlockSpec((block_side, feature_count), tile_map_of(slot)) for slot in range(group)],
        out_specs=pl.BlockSpec((target_blocks * block_side, feature_count), out_map),
        scratch_shapes=[pltpu.VMEM((target_blocks, block_side, feature_count), jnp.float32)],
    )
    return pl.pallas_call(
        functools.partial(block_kernel, transpose=transpose),
        grid_spec=grid_spec,
        out_shape=jax.ShapeDtypeStruct((target_blocks * block_side, feature_count), jnp.bfloat16),
        compiler_params=pltpu.CompilerParams(dimension_semantics=("arbitrary",)),
    )(source_ids, target_ids, live, values, *([source] * group))


ROW = ("zl", "x", "core")
COL = ("zh", "y")


def exchange_sum(parts, axis_name, count):
    pieces = parts.reshape((count, -1) + parts.shape[1:])
    pieces = lax.all_to_all(pieces, axis_name, 0, 0, tiled=False)
    return pieces.astype(jnp.float32).sum(0)


def staged_sum(parts, axes, sizes):
    pieces = parts.reshape(tuple(sizes) + (-1,) + parts.shape[1:])
    for position in reversed(range(len(axes))):
        pieces = lax.all_to_all(pieces, axes[position], position, position, tiled=False)
        pieces = pieces.astype(jnp.float32).sum(position)
        if position > 0:
            pieces = pieces.astype(jnp.bfloat16)
    return pieces


def exchange_gather(part, axis_name, count):
    pieces = jnp.broadcast_to(part[None], (count,) + part.shape)
    pieces = lax.all_to_all(pieces, axis_name, 0, 0, tiled=False)
    return pieces.reshape((-1,) + part.shape[1:])


def silu_slope(summed):
    sigmoid_value = jax.nn.sigmoid(summed)
    return sigmoid_value * (1.0 + summed * (1.0 - sigmoid_value))


def shards(features, weight, entry_values, block_rows, block_cols, entry_counts, cotangent):
    values = entry_values[0, 0]
    row_ids = block_rows[0, 0]
    col_ids = block_cols[0, 0]
    live_count = entry_counts[0, 0]
    local_rows = features.shape[0]
    block_side = values.shape[1]
    row_sizes = [lax.axis_size(name) for name in ROW]
    col_sizes = [lax.axis_size(name) for name in COL]
    row_count = row_sizes[0] * row_sizes[1] * row_sizes[2]
    col_count = col_sizes[0] * col_sizes[1]
    row_span = col_count * local_rows
    col_span = row_count * local_rows
    panel = lax.all_gather(features, ROW, axis=0, tiled=True)
    forward_terms = block_terms(
        values, col_ids, row_ids, live_count, panel, row_span // block_side, False
    )
    own_mixed = staged_sum(forward_terms, COL, col_sizes).astype(jnp.bfloat16)
    own_sum = jnp.dot(own_mixed, weight, preferred_element_type=jnp.float32)
    output = jax.nn.silu(own_sum).astype(jnp.bfloat16)
    own_upstream = (cotangent.astype(jnp.float32) * silu_slope(own_sum)).astype(jnp.bfloat16)
    weight_term = lax.dot_general(
        own_mixed, own_upstream, (((0,), (0,)), ((), ())), preferred_element_type=jnp.float32
    )
    weight_part = exchange_sum(exchange_sum(weight_term, ROW, row_count), COL, col_count)
    grad_weight = exchange_gather(exchange_gather(weight_part, COL, col_count), ROW, row_count)
    upstream = lax.all_gather(own_upstream, COL, axis=0, tiled=True)
    upstream, grad_weight = lax.optimization_barrier((upstream, grad_weight))
    backward_terms = block_terms(
        values, row_ids, col_ids, live_count, upstream, col_span // block_side, True
    )
    grad_projected = staged_sum(backward_terms, ROW, row_sizes).astype(jnp.bfloat16)
    grad_features = lax.dot_general(
        grad_projected, weight, (((1,), (1,)), ((), ())), preferred_element_type=jnp.float32
    ).astype(jnp.bfloat16)
    return (output, grad_features, grad_weight)


def solution(mesh):
    row_parts = (2, 4, 2)
    col_parts = (4, 4)
    split = Mesh(mesh.devices.reshape(row_parts + col_parts), ROW + COL)
    placed = (
        P(COL + ROW, None),
        P(),
        P(ROW, COL, None, None, None),
        P(ROW, COL, None),
        P(ROW, COL, None),
        P(ROW, COL),
        P(ROW + COL, None),
    )
    return jax.shard_map(
        shards,
        mesh=split,
        in_specs=placed,
        out_specs=(P(ROW + COL, None), P(COL + ROW, None), P()),
        check_vma=False,
    )
```

```python
import functools
import jax
import jax.numpy as jnp
from jax import lax
from jax.experimental import pallas as pl
from jax.experimental.pallas import tpu as pltpu
from jax.sharding import Mesh, PartitionSpec as P

GROUP = 4


def block_kernel(source_ids, target_ids, live, values_ref, *refs, transpose):
    tile_refs, out_ref, acc_ref = refs[:-2], refs[-2], refs[-1]
    step = pl.program_id(0)
    group = len(tile_refs)

    @pl.when(step == 0)
    def _():
        acc_ref[...] = jnp.zeros_like(acc_ref)

    for slot, tile_ref in enumerate(tile_refs):
        entry = step * group + slot

        @pl.when(entry < live[0])
        def _():
            block = values_ref[slot]
            if transpose:
                term = lax.dot_general(block, tile_ref[...], (((0,), (0,)), ((), ())), preferred_element_type=jnp.float32)
            else:
                term = jnp.dot(block, tile_ref[...], preferred_element_type=jnp.float32)
            acc_ref[target_ids[entry]] += term

    @pl.when(step == pl.num_programs(0) - 1)
    def _():
        out_ref[...] = acc_ref[...].reshape(out_ref.shape).astype(out_ref.dtype)


def block_terms(values, source_ids, target_ids, live_count, source, target_blocks, transpose):
    entry_total, block_side, _ = values.shape
    feature_count = source.shape[1]
    group = GROUP
    live = jnp.reshape(live_count, (1,)).astype(jnp.int32)

    def values_map(step, source_ids, target_ids, live):
        return (jnp.minimum(step, (live[0] - 1) // group), 0, 0)

    def tile_map_of(slot):
        def tile_map(step, source_ids, target_ids, live):
            return (source_ids[jnp.minimum(step * group + slot, live[0] - 1)], 0)
        return tile_map

    def out_map(step, source_ids, target_ids, live):
        return (0, 0)

    grid_spec = pltpu.PrefetchScalarGridSpec(
        num_scalar_prefetch=3,
        grid=(entry_total // group,),
        in_specs=[pl.BlockSpec((group, block_side, block_side), values_map)]
        + [pl.BlockSpec((block_side, feature_count), tile_map_of(slot)) for slot in range(group)],
        out_specs=pl.BlockSpec((target_blocks * block_side, feature_count), out_map),
        scratch_shapes=[pltpu.VMEM((target_blocks, block_side, feature_count), jnp.float32)],
    )
    return pl.pallas_call(
        functools.partial(block_kernel, transpose=transpose),
        grid_spec=grid_spec,
        out_shape=jax.ShapeDtypeStruct((target_blocks * block_side, feature_count), jnp.bfloat16),
        compiler_params=pltpu.CompilerParams(dimension_semantics=("arbitrary",)),
    )(source_ids, target_ids, live, values, *([source] * group))


ROW = ("zl", "x", "core")
COL = ("zh", "y")


def exchange_sum(parts, axis_name, count):
    pieces = parts.reshape((count, -1) + parts.shape[1:])
    pieces = lax.all_to_all(pieces, axis_name, 0, 0, tiled=False)
    return pieces.astype(jnp.float32).sum(0)


def reversed_blocks(target_ids, sizes, blocks_per_part):
    part, half = target_ids // blocks_per_part, target_ids % blocks_per_part
    flipped, stride = 0, 1
    for size in reversed(sizes):
        flipped = flipped * size + part % size
        part = part // size
    return flipped * blocks_per_part + half


def staged_sum(parts, axes, sizes):
    pieces = parts.reshape(tuple(reversed(sizes)) + (-1,) + parts.shape[1:])
    for position, name in enumerate(reversed(axes)):
        pieces = lax.all_to_all(pieces, name, 0, 0, tiled=False)
        pieces = pieces.astype(jnp.float32).sum(0)
        if position < len(axes) - 1:
            pieces = pieces.astype(jnp.bfloat16)
    return pieces


def exchange_gather(part, axis_name, count):
    pieces = jnp.broadcast_to(part[None], (count,) + part.shape)
    pieces = lax.all_to_all(pieces, axis_name, 0, 0, tiled=False)
    return pieces.reshape((-1,) + part.shape[1:])


def silu_slope(summed):
    sigmoid_value = jax.nn.sigmoid(summed)
    return sigmoid_value * (1.0 + summed * (1.0 - sigmoid_value))


def shards(features, weight, entry_values, block_rows, block_cols, entry_counts, cotangent):
    values = entry_values[0, 0]
    row_ids = block_rows[0, 0]
    col_ids = block_cols[0, 0]
    live_count = entry_counts[0, 0]
    local_rows = features.shape[0]
    block_side = values.shape[1]
    row_sizes = [lax.axis_size(name) for name in ROW]
    col_sizes = [lax.axis_size(name) for name in COL]
    row_count = row_sizes[0] * row_sizes[1] * row_sizes[2]
    col_count = col_sizes[0] * col_sizes[1]
    row_span = col_count * local_rows
    col_span = row_count * local_rows
    panel = lax.all_gather(features, ROW, axis=0, tiled=True)
    parts_per_device = local_rows // block_side
    forward_terms = block_terms(
        values, col_ids, reversed_blocks(row_ids, col_sizes, parts_per_device), live_count,
        panel, row_span // block_side, False
    )
    own_mixed = staged_sum(forward_terms, COL, col_sizes).astype(jnp.bfloat16)
    own_sum = jnp.dot(own_mixed, weight, preferred_element_type=jnp.float32)
    output = jax.nn.silu(own_sum).astype(jnp.bfloat16)
    own_upstream = (cotangent.astype(jnp.float32) * silu_slope(own_sum)).astype(jnp.bfloat16)
    weight_term = lax.dot_general(
        own_mixed, own_upstream, (((0,), (0,)), ((), ())), preferred_element_type=jnp.float32
    )
    weight_part = exchange_sum(exchange_sum(weight_term, ROW, row_count), COL, col_count)
    grad_weight = exchange_gather(exchange_gather(weight_part, COL, col_count), ROW, row_count)
    upstream = lax.all_gather(own_upstream, COL, axis=0, tiled=True)
    upstream, grad_weight = lax.optimization_barrier((upstream, grad_weight))
    backward_terms = block_terms(
        values, row_ids, reversed_blocks(col_ids, row_sizes, parts_per_device), live_count,
        upstream, col_span // block_side, True
    )
    grad_projected = staged_sum(backward_terms, ROW, row_sizes).astype(jnp.bfloat16)
    grad_features = lax.dot_general(
        grad_projected, weight, (((1,), (1,)), ((), ())), preferred_element_type=jnp.float32
    ).astype(jnp.bfloat16)
    return (output, grad_features, grad_weight)


def solution(mesh):
    row_parts = (2, 4, 2)
    col_parts = (4, 4)
    split = Mesh(mesh.devices.reshape(row_parts + col_parts), ROW + COL)
    placed = (
        P(COL + ROW, None),
        P(),
        P(ROW, COL, None, None, None),
        P(ROW, COL, None),
        P(ROW, COL, None),
        P(ROW, COL),
        P(ROW + COL, None),
    )
    return jax.shard_map(
        shards,
        mesh=split,
        in_specs=placed,
        out_specs=(P(ROW + COL, None), P(COL + ROW, None), P()),
        check_vma=False,
    )
```

```python
import functools
import jax
import jax.numpy as jnp
from jax import lax
from jax.experimental import pallas as pl
from jax.experimental.pallas import tpu as pltpu
from jax.sharding import Mesh, PartitionSpec as P

GROUP = 4


def block_kernel(source_ids, target_ids, live, values_ref, *refs, transpose):
    tile_refs, out_ref, acc_ref = refs[:-2], refs[-2], refs[-1]
    step = pl.program_id(0)
    group = len(tile_refs)

    @pl.when(step == 0)
    def _():
        acc_ref[...] = jnp.zeros_like(acc_ref)

    for slot, tile_ref in enumerate(tile_refs):
        entry = step * group + slot

        @pl.when(entry < live[0])
        def _():
            block = values_ref[slot]
            if transpose:
                term = lax.dot_general(block, tile_ref[...], (((0,), (0,)), ((), ())), preferred_element_type=jnp.float32)
            else:
                term = jnp.dot(block, tile_ref[...], preferred_element_type=jnp.float32)
            acc_ref[target_ids[entry]] += term

    @pl.when(step == pl.num_programs(0) - 1)
    def _():
        out_ref[...] = acc_ref[...].reshape(out_ref.shape).astype(out_ref.dtype)


def block_terms(values, source_ids, target_ids, live_count, source, target_blocks, transpose):
    entry_total, block_side, _ = values.shape
    feature_count = source.shape[1]
    group = GROUP
    live = jnp.reshape(live_count, (1,)).astype(jnp.int32)

    def values_map(step, source_ids, target_ids, live):
        return (jnp.minimum(step, (live[0] - 1) // group), 0, 0)

    def tile_map_of(slot):
        def tile_map(step, source_ids, target_ids, live):
            return (source_ids[jnp.minimum(step * group + slot, live[0] - 1)], 0)
        return tile_map

    def out_map(step, source_ids, target_ids, live):
        return (0, 0)

    grid_spec = pltpu.PrefetchScalarGridSpec(
        num_scalar_prefetch=3,
        grid=(entry_total // group,),
        in_specs=[pl.BlockSpec((group, block_side, block_side), values_map)]
        + [pl.BlockSpec((block_side, feature_count), tile_map_of(slot)) for slot in range(group)],
        out_specs=pl.BlockSpec((target_blocks * block_side, feature_count), out_map),
        scratch_shapes=[pltpu.VMEM((target_blocks, block_side, feature_count), jnp.float32)],
    )
    return pl.pallas_call(
        functools.partial(block_kernel, transpose=transpose),
        grid_spec=grid_spec,
        out_shape=jax.ShapeDtypeStruct((target_blocks * block_side, feature_count), jnp.bfloat16),
        compiler_params=pltpu.CompilerParams(dimension_semantics=("arbitrary",)),
    )(source_ids, target_ids, live, values, *([source] * group))


ROW = ("zl", "x", "core")
COL = ("zh", "y")


def exchange_sum(parts, axis_name, count):
    pieces = parts.reshape((count, -1) + parts.shape[1:])
    pieces = lax.all_to_all(pieces, axis_name, 0, 0, tiled=False)
    return pieces.astype(jnp.float32).sum(0)


def reversed_blocks(target_ids, sizes, blocks_per_part):
    part, half = target_ids // blocks_per_part, target_ids % blocks_per_part
    flipped, stride = 0, 1
    for size in reversed(sizes):
        flipped = flipped * size + part % size
        part = part // size
    return flipped * blocks_per_part + half


def staged_sum(parts, axes, sizes):
    pieces = parts.reshape(tuple(reversed(sizes)) + (-1,) + parts.shape[1:])
    for position, name in enumerate(reversed(axes)):
        pieces = lax.all_to_all(pieces, name, 0, 0, tiled=False)
        pieces = pieces.astype(jnp.float32).sum(0)
        if position < len(axes) - 1:
            pieces = pieces.astype(jnp.bfloat16)
    return pieces


def exchange_gather(part, axis_name, count):
    pieces = jnp.broadcast_to(part[None], (count,) + part.shape)
    pieces = lax.all_to_all(pieces, axis_name, 0, 0, tiled=False)
    return pieces.reshape((-1,) + part.shape[1:])


def silu_slope(summed):
    sigmoid_value = jax.nn.sigmoid(summed)
    return sigmoid_value * (1.0 + summed * (1.0 - sigmoid_value))


def shards(features, weight, entry_values, block_rows, block_cols, entry_counts, cotangent):
    values = entry_values[0, 0]
    row_ids = block_rows[0, 0]
    col_ids = block_cols[0, 0]
    live_count = entry_counts[0, 0]
    local_rows = features.shape[0]
    block_side = values.shape[1]
    row_sizes = [lax.axis_size(name) for name in ROW]
    col_sizes = [lax.axis_size(name) for name in COL]
    row_count = row_sizes[0] * row_sizes[1] * row_sizes[2]
    col_count = col_sizes[0] * col_sizes[1]
    row_span = col_count * local_rows
    col_span = row_count * local_rows
    panel = exchange_gather(features, ROW, row_count)
    parts_per_device = local_rows // block_side
    forward_terms = block_terms(
        values, col_ids, reversed_blocks(row_ids, col_sizes, parts_per_device), live_count,
        panel, row_span // block_side, False
    )
    own_mixed = staged_sum(forward_terms, COL, col_sizes).astype(jnp.bfloat16)
    own_sum = jnp.dot(own_mixed, weight, preferred_element_type=jnp.float32)
    output = jax.nn.silu(own_sum).astype(jnp.bfloat16)
    own_upstream = (cotangent.astype(jnp.float32) * silu_slope(own_sum)).astype(jnp.bfloat16)
    weight_term = lax.dot_general(
        own_mixed, own_upstream, (((0,), (0,)), ((), ())), preferred_element_type=jnp.float32
    )
    weight_part = exchange_sum(weight_term, ROW, row_count)
    weight_part = exchange_gather(weight_part[None], COL, col_count).sum(0)
    grad_weight = exchange_gather(weight_part, ROW, row_count)
    upstream = lax.all_gather(own_upstream, COL, axis=0, tiled=True)
    upstream, grad_weight = lax.optimization_barrier((upstream, grad_weight))
    backward_terms = block_terms(
        values, row_ids, reversed_blocks(col_ids, row_sizes, parts_per_device), live_count,
        upstream, col_span // block_side, True
    )
    grad_projected = staged_sum(backward_terms, ROW, row_sizes).astype(jnp.bfloat16)
    grad_features = lax.dot_general(
        grad_projected, weight, (((1,), (1,)), ((), ())), preferred_element_type=jnp.float32
    ).astype(jnp.bfloat16)
    return (output, grad_features, grad_weight)


def solution(mesh):
    row_parts = (2, 4, 2)
    col_parts = (4, 4)
    split = Mesh(mesh.devices.reshape(row_parts + col_parts), ROW + COL)
    placed = (
        P(COL + ROW, None),
        P(),
        P(ROW, COL, None, None, None),
        P(ROW, COL, None),
        P(ROW, COL, None),
        P(ROW, COL),
        P(ROW + COL, None),
    )
    return jax.shard_map(
        shards,
        mesh=split,
        in_specs=placed,
        out_specs=(P(ROW + COL, None), P(COL + ROW, None), P()),
        check_vma=False,
    )
```

```python
import functools
import jax
import jax.numpy as jnp
from jax import lax
from jax.experimental import pallas as pl
from jax.experimental.pallas import tpu as pltpu
from jax.sharding import Mesh, PartitionSpec as P

GROUP = 8


def block_kernel(source_ids, target_ids, live, values_ref, *refs, transpose):
    tile_refs, out_ref, acc_ref = refs[:-2], refs[-2], refs[-1]
    step = pl.program_id(0)
    group = len(tile_refs)

    @pl.when(step == 0)
    def _():
        acc_ref[...] = jnp.zeros_like(acc_ref)

    for slot, tile_ref in enumerate(tile_refs):
        entry = step * group + slot

        @pl.when(entry < live[0])
        def _():
            block = values_ref[slot]
            if transpose:
                term = lax.dot_general(block, tile_ref[...], (((0,), (0,)), ((), ())), preferred_element_type=jnp.float32)
            else:
                term = jnp.dot(block, tile_ref[...], preferred_element_type=jnp.float32)
            acc_ref[target_ids[entry]] += term

    @pl.when(step == pl.num_programs(0) - 1)
    def _():
        out_ref[...] = acc_ref[...].reshape(out_ref.shape).astype(out_ref.dtype)


def block_terms(values, source_ids, target_ids, live_count, source, target_blocks, transpose):
    entry_total, block_side, _ = values.shape
    feature_count = source.shape[1]
    group = GROUP
    live = jnp.reshape(live_count, (1,)).astype(jnp.int32)

    def values_map(step, source_ids, target_ids, live):
        return (jnp.minimum(step, (live[0] - 1) // group), 0, 0)

    def tile_map_of(slot):
        def tile_map(step, source_ids, target_ids, live):
            return (source_ids[jnp.minimum(step * group + slot, live[0] - 1)], 0)
        return tile_map

    def out_map(step, source_ids, target_ids, live):
        return (0, 0)

    grid_spec = pltpu.PrefetchScalarGridSpec(
        num_scalar_prefetch=3,
        grid=(entry_total // group,),
        in_specs=[pl.BlockSpec((group, block_side, block_side), values_map)]
        + [pl.BlockSpec((block_side, feature_count), tile_map_of(slot)) for slot in range(group)],
        out_specs=pl.BlockSpec((target_blocks * block_side, feature_count), out_map),
        scratch_shapes=[pltpu.VMEM((target_blocks, block_side, feature_count), jnp.float32)],
    )
    return pl.pallas_call(
        functools.partial(block_kernel, transpose=transpose),
        grid_spec=grid_spec,
        out_shape=jax.ShapeDtypeStruct((target_blocks * block_side, feature_count), jnp.bfloat16),
        compiler_params=pltpu.CompilerParams(dimension_semantics=("arbitrary",)),
    )(source_ids, target_ids, live, values, *([source] * group))


ROW = ("zl", "x", "core")
COL = ("zh", "y")


def exchange_sum(parts, axis_name, count):
    pieces = parts.reshape((count, -1) + parts.shape[1:])
    pieces = lax.all_to_all(pieces, axis_name, 0, 0, tiled=False)
    return pieces.astype(jnp.float32).sum(0)


def reversed_blocks(target_ids, sizes, blocks_per_part):
    part, half = target_ids // blocks_per_part, target_ids % blocks_per_part
    flipped, stride = 0, 1
    for size in reversed(sizes):
        flipped = flipped * size + part % size
        part = part // size
    return flipped * blocks_per_part + half


def staged_sum(parts, axes, sizes):
    pieces = parts.reshape(tuple(reversed(sizes)) + (-1,) + parts.shape[1:])
    for position, name in enumerate(reversed(axes)):
        pieces = lax.all_to_all(pieces, name, 0, 0, tiled=False)
        pieces = pieces.astype(jnp.float32).sum(0)
        if position < len(axes) - 1:
            pieces = pieces.astype(jnp.bfloat16)
    return pieces


def exchange_gather(part, axis_name, count):
    pieces = jnp.broadcast_to(part[None], (count,) + part.shape)
    pieces = lax.all_to_all(pieces, axis_name, 0, 0, tiled=False)
    return pieces.reshape((-1,) + part.shape[1:])


def silu_slope(summed):
    sigmoid_value = jax.nn.sigmoid(summed)
    return sigmoid_value * (1.0 + summed * (1.0 - sigmoid_value))


def shards(features, weight, entry_values, block_rows, block_cols, entry_counts, cotangent):
    values = entry_values[0, 0]
    row_ids = block_rows[0, 0]
    col_ids = block_cols[0, 0]
    live_count = entry_counts[0, 0]
    local_rows = features.shape[0]
    block_side = values.shape[1]
    row_sizes = [lax.axis_size(name) for name in ROW]
    col_sizes = [lax.axis_size(name) for name in COL]
    row_count = row_sizes[0] * row_sizes[1] * row_sizes[2]
    col_count = col_sizes[0] * col_sizes[1]
    row_span = col_count * local_rows
    col_span = row_count * local_rows
    panel = lax.all_gather(features, ROW, axis=0, tiled=True)
    parts_per_device = local_rows // block_side
    forward_terms = block_terms(
        values, col_ids, reversed_blocks(row_ids, col_sizes, parts_per_device), live_count,
        panel, row_span // block_side, False
    )
    own_mixed = staged_sum(forward_terms, COL, col_sizes).astype(jnp.bfloat16)
    own_sum = jnp.dot(own_mixed, weight, preferred_element_type=jnp.float32)
    output = jax.nn.silu(own_sum).astype(jnp.bfloat16)
    own_upstream = (cotangent.astype(jnp.float32) * silu_slope(own_sum)).astype(jnp.bfloat16)
    weight_term = lax.dot_general(
        own_mixed, own_upstream, (((0,), (0,)), ((), ())), preferred_element_type=jnp.float32
    )
    weight_part = exchange_sum(exchange_sum(weight_term, ROW, row_count), COL, col_count)
    grad_weight = exchange_gather(exchange_gather(weight_part, COL, col_count), ROW, row_count)
    upstream = lax.all_gather(own_upstream, COL, axis=0, tiled=True)
    upstream, grad_weight = lax.optimization_barrier((upstream, grad_weight))
    backward_terms = block_terms(
        values, row_ids, reversed_blocks(col_ids, row_sizes, parts_per_device), live_count,
        upstream, col_span // block_side, True
    )
    grad_projected = staged_sum(backward_terms, ROW, row_sizes).astype(jnp.bfloat16)
    grad_features = lax.dot_general(
        grad_projected, weight, (((1,), (1,)), ((), ())), preferred_element_type=jnp.float32
    ).astype(jnp.bfloat16)
    return (output, grad_features, grad_weight)


def solution(mesh):
    row_parts = (2, 4, 2)
    col_parts = (4, 4)
    split = Mesh(mesh.devices.reshape(row_parts + col_parts), ROW + COL)
    placed = (
        P(COL + ROW, None),
        P(),
        P(ROW, COL, None, None, None),
        P(ROW, COL, None),
        P(ROW, COL, None),
        P(ROW, COL),
        P(ROW + COL, None),
    )
    return jax.shard_map(
        shards,
        mesh=split,
        in_specs=placed,
        out_specs=(P(ROW + COL, None), P(COL + ROW, None), P()),
        check_vma=False,
    )
```

```python
import functools
import jax
import jax.numpy as jnp
from jax import lax
from jax.experimental import pallas as pl
from jax.experimental.pallas import tpu as pltpu
from jax.sharding import Mesh, PartitionSpec as P

GROUP = 8


def block_kernel(source_ids, target_ids, live, values_ref, *refs, transpose):
    tile_refs, out_ref, acc_ref, seen_ref = refs[:-3], refs[-3], refs[-2], refs[-1]
    step = pl.program_id(0)
    group = len(tile_refs)
    block_count, block_side, _ = acc_ref.shape

    @pl.when(step == 0)
    def _():
        for block in range(block_count):
            seen_ref[block] = 0

    for slot, tile_ref in enumerate(tile_refs):
        entry = step * group + slot

        @pl.when(entry < live[0])
        def _():
            block = values_ref[slot]
            if transpose:
                term = lax.dot_general(block, tile_ref[...], (((0,), (0,)), ((), ())), preferred_element_type=jnp.float32)
            else:
                term = jnp.dot(block, tile_ref[...], preferred_element_type=jnp.float32)
            target = target_ids[entry]
            fresh = seen_ref[target] == 0

            @pl.when(fresh)
            def _():
                acc_ref[target] = term

            @pl.when(jnp.logical_not(fresh))
            def _():
                acc_ref[target] += term

            seen_ref[target] = 1

    @pl.when(step == pl.num_programs(0) - 1)
    def _():
        for block in range(block_count):
            rows = pl.ds(block * block_side, block_side)
            touched = seen_ref[block] != 0

            @pl.when(touched)
            def _():
                out_ref[rows, :] = acc_ref[block].astype(out_ref.dtype)

            @pl.when(jnp.logical_not(touched))
            def _():
                out_ref[rows, :] = jnp.zeros((block_side, out_ref.shape[1]), out_ref.dtype)


def block_terms(values, source_ids, target_ids, live_count, source, target_blocks, transpose):
    entry_total, block_side, _ = values.shape
    feature_count = source.shape[1]
    group = GROUP
    live = jnp.reshape(live_count, (1,)).astype(jnp.int32)

    def values_map(step, source_ids, target_ids, live):
        return (jnp.minimum(step, (live[0] - 1) // group), 0, 0)

    def tile_map_of(slot):
        def tile_map(step, source_ids, target_ids, live):
            return (source_ids[jnp.minimum(step * group + slot, live[0] - 1)], 0)
        return tile_map

    def out_map(step, source_ids, target_ids, live):
        return (0, 0)

    grid_spec = pltpu.PrefetchScalarGridSpec(
        num_scalar_prefetch=3,
        grid=(entry_total // group,),
        in_specs=[pl.BlockSpec((group, block_side, block_side), values_map)]
        + [pl.BlockSpec((block_side, feature_count), tile_map_of(slot)) for slot in range(group)],
        out_specs=pl.BlockSpec((target_blocks * block_side, feature_count), out_map),
        scratch_shapes=[
            pltpu.VMEM((target_blocks, block_side, feature_count), jnp.float32),
            pltpu.SMEM((target_blocks,), jnp.int32),
        ],
    )
    return pl.pallas_call(
        functools.partial(block_kernel, transpose=transpose),
        grid_spec=grid_spec,
        out_shape=jax.ShapeDtypeStruct((target_blocks * block_side, feature_count), jnp.bfloat16),
        compiler_params=pltpu.CompilerParams(dimension_semantics=("arbitrary",)),
    )(source_ids, target_ids, live, values, *([source] * group))


ROW = ("zl", "x", "core")
COL = ("zh", "y")


def exchange_sum(parts, axis_name, count):
    pieces = parts.reshape((count, -1) + parts.shape[1:])
    pieces = lax.all_to_all(pieces, axis_name, 0, 0, tiled=False)
    return pieces.astype(jnp.float32).sum(0)


def reversed_blocks(target_ids, sizes, blocks_per_part):
    part, half = target_ids // blocks_per_part, target_ids % blocks_per_part
    flipped, stride = 0, 1
    for size in reversed(sizes):
        flipped = flipped * size + part % size
        part = part // size
    return flipped * blocks_per_part + half


def staged_sum(parts, axes, sizes):
    pieces = parts.reshape(tuple(reversed(sizes)) + (-1,) + parts.shape[1:])
    for position, name in enumerate(reversed(axes)):
        pieces = lax.all_to_all(pieces, name, 0, 0, tiled=False)
        pieces = pieces.astype(jnp.float32).sum(0)
        if position < len(axes) - 1:
            pieces = pieces.astype(jnp.bfloat16)
    return pieces


def exchange_gather(part, axis_name, count):
    pieces = jnp.broadcast_to(part[None], (count,) + part.shape)
    pieces = lax.all_to_all(pieces, axis_name, 0, 0, tiled=False)
    return pieces.reshape((-1,) + part.shape[1:])


def silu_slope(summed):
    sigmoid_value = jax.nn.sigmoid(summed)
    return sigmoid_value * (1.0 + summed * (1.0 - sigmoid_value))


def shards(features, weight, entry_values, block_rows, block_cols, entry_counts, cotangent):
    values = entry_values[0, 0]
    row_ids = block_rows[0, 0]
    col_ids = block_cols[0, 0]
    live_count = entry_counts[0, 0]
    local_rows = features.shape[0]
    block_side = values.shape[1]
    row_sizes = [lax.axis_size(name) for name in ROW]
    col_sizes = [lax.axis_size(name) for name in COL]
    row_count = row_sizes[0] * row_sizes[1] * row_sizes[2]
    col_count = col_sizes[0] * col_sizes[1]
    row_span = col_count * local_rows
    col_span = row_count * local_rows
    panel = lax.all_gather(features, ROW, axis=0, tiled=True)
    parts_per_device = local_rows // block_side
    forward_terms = block_terms(
        values, col_ids, reversed_blocks(row_ids, col_sizes, parts_per_device), live_count,
        panel, row_span // block_side, False
    )
    own_mixed = staged_sum(forward_terms, COL, col_sizes).astype(jnp.bfloat16)
    own_sum = jnp.dot(own_mixed, weight, preferred_element_type=jnp.float32)
    output = jax.nn.silu(own_sum).astype(jnp.bfloat16)
    own_upstream = (cotangent.astype(jnp.float32) * silu_slope(own_sum)).astype(jnp.bfloat16)
    weight_term = lax.dot_general(
        own_mixed, own_upstream, (((0,), (0,)), ((), ())), preferred_element_type=jnp.float32
    )
    weight_part = exchange_sum(exchange_sum(weight_term, ROW, row_count), COL, col_count)
    grad_weight = exchange_gather(exchange_gather(weight_part, COL, col_count), ROW, row_count)
    upstream = lax.all_gather(own_upstream, COL, axis=0, tiled=True)
    upstream, grad_weight = lax.optimization_barrier((upstream, grad_weight))
    backward_terms = block_terms(
        values, row_ids, reversed_blocks(col_ids, row_sizes, parts_per_device), live_count,
        upstream, col_span // block_side, True
    )
    grad_projected = staged_sum(backward_terms, ROW, row_sizes).astype(jnp.bfloat16)
    grad_features = lax.dot_general(
        grad_projected, weight, (((1,), (1,)), ((), ())), preferred_element_type=jnp.float32
    ).astype(jnp.bfloat16)
    return (output, grad_features, grad_weight)


def solution(mesh):
    row_parts = (2, 4, 2)
    col_parts = (4, 4)
    split = Mesh(mesh.devices.reshape(row_parts + col_parts), ROW + COL)
    placed = (
        P(COL + ROW, None),
        P(),
        P(ROW, COL, None, None, None),
        P(ROW, COL, None),
        P(ROW, COL, None),
        P(ROW, COL),
        P(ROW + COL, None),
    )
    return jax.shard_map(
        shards,
        mesh=split,
        in_specs=placed,
        out_specs=(P(ROW + COL, None), P(COL + ROW, None), P()),
        check_vma=False,
    )
```

```python
import functools
import jax
import jax.numpy as jnp
from jax import lax
from jax.experimental import pallas as pl
from jax.experimental.pallas import tpu as pltpu
from jax.sharding import Mesh, PartitionSpec as P

GROUP = 8


def block_kernel(source_ids, target_ids, live, values_ref, *refs, transpose):
    tile_refs, out_ref, acc_ref, seen_ref = refs[:-3], refs[-3], refs[-2], refs[-1]
    step = pl.program_id(0)
    group = len(tile_refs)
    block_count, block_side, _ = acc_ref.shape

    @pl.when(step == 0)
    def _():
        for block in range(block_count):
            seen_ref[block] = 0

    for slot, tile_ref in enumerate(tile_refs):
        entry = step * group + slot

        @pl.when(entry < live[0])
        def _():
            block = values_ref[slot]
            if transpose:
                term = lax.dot_general(block, tile_ref[...], (((0,), (0,)), ((), ())), preferred_element_type=jnp.float32)
            else:
                term = jnp.dot(block, tile_ref[...], preferred_element_type=jnp.float32)
            target = target_ids[entry]
            fresh = seen_ref[target] == 0

            @pl.when(fresh)
            def _():
                acc_ref[target] = term

            @pl.when(jnp.logical_not(fresh))
            def _():
                acc_ref[target] += term

            seen_ref[target] = 1

    @pl.when(step == pl.num_programs(0) - 1)
    def _():
        for block in range(block_count):
            rows = pl.ds(block * block_side, block_side)
            touched = seen_ref[block] != 0

            @pl.when(touched)
            def _():
                out_ref[rows, :] = acc_ref[block].astype(out_ref.dtype)

            @pl.when(jnp.logical_not(touched))
            def _():
                out_ref[rows, :] = jnp.zeros((block_side, out_ref.shape[1]), out_ref.dtype)


def block_terms(values, source_ids, target_ids, live_count, source, target_blocks, transpose):
    entry_total, block_side, _ = values.shape
    feature_count = source.shape[1]
    group = GROUP
    live = jnp.reshape(live_count, (1,)).astype(jnp.int32)

    def values_map(step, source_ids, target_ids, live):
        return (jnp.minimum(step, (live[0] - 1) // group), 0, 0)

    def tile_map_of(slot):
        def tile_map(step, source_ids, target_ids, live):
            return (source_ids[jnp.minimum(step * group + slot, live[0] - 1)], 0)
        return tile_map

    def out_map(step, source_ids, target_ids, live):
        return (0, 0)

    grid_spec = pltpu.PrefetchScalarGridSpec(
        num_scalar_prefetch=3,
        grid=(entry_total // group,),
        in_specs=[pl.BlockSpec((group, block_side, block_side), values_map)]
        + [pl.BlockSpec((block_side, feature_count), tile_map_of(slot)) for slot in range(group)],
        out_specs=pl.BlockSpec((target_blocks * block_side, feature_count), out_map),
        scratch_shapes=[
            pltpu.VMEM((target_blocks, block_side, feature_count), jnp.float32),
            pltpu.SMEM((target_blocks,), jnp.int32),
        ],
    )
    return pl.pallas_call(
        functools.partial(block_kernel, transpose=transpose),
        grid_spec=grid_spec,
        out_shape=jax.ShapeDtypeStruct((target_blocks * block_side, feature_count), jnp.bfloat16),
        compiler_params=pltpu.CompilerParams(dimension_semantics=("arbitrary",)),
    )(source_ids, target_ids, live, values, *([source] * group))


ROW = ("zl", "x", "core")
COL = ("zh", "y")


def exchange_sum(parts, axis_name, count):
    pieces = parts.reshape((count, -1) + parts.shape[1:])
    pieces = lax.all_to_all(pieces, axis_name, 0, 0, tiled=False)
    return pieces.astype(jnp.float32).sum(0)


def reversed_blocks(target_ids, sizes, blocks_per_part):
    part, half = target_ids // blocks_per_part, target_ids % blocks_per_part
    flipped, stride = 0, 1
    for size in reversed(sizes):
        flipped = flipped * size + part % size
        part = part // size
    return flipped * blocks_per_part + half


def staged_sum(parts, axes, sizes):
    pieces = parts.reshape(tuple(reversed(sizes)) + (-1,) + parts.shape[1:])
    for position, name in enumerate(reversed(axes)):
        pieces = lax.all_to_all(pieces, name, 0, 0, tiled=False)
        pieces = pieces.astype(jnp.float32).sum(0)
        if position < len(axes) - 1:
            pieces = pieces.astype(jnp.bfloat16)
    return pieces


def exchange_gather(part, axis_name, count):
    pieces = jnp.broadcast_to(part[None], (count,) + part.shape)
    pieces = lax.all_to_all(pieces, axis_name, 0, 0, tiled=False)
    return pieces.reshape((-1,) + part.shape[1:])


def silu_slope(summed):
    sigmoid_value = jax.nn.sigmoid(summed)
    return sigmoid_value * (1.0 + summed * (1.0 - sigmoid_value))


def shards(features, weight, entry_values, block_rows, block_cols, entry_counts, cotangent):
    values = entry_values[0, 0]
    row_ids = block_rows[0, 0]
    col_ids = block_cols[0, 0]
    live_count = entry_counts[0, 0]
    local_rows = features.shape[0]
    block_side = values.shape[1]
    row_sizes = [lax.axis_size(name) for name in ROW]
    col_sizes = [lax.axis_size(name) for name in COL]
    row_count = row_sizes[0] * row_sizes[1] * row_sizes[2]
    col_count = col_sizes[0] * col_sizes[1]
    row_span = col_count * local_rows
    col_span = row_count * local_rows
    panel = lax.all_gather(features, ROW, axis=0, tiled=True)
    parts_per_device = local_rows // block_side
    forward_terms = block_terms(
        values, col_ids, reversed_blocks(row_ids, col_sizes, parts_per_device), live_count,
        panel, row_span // block_side, False
    )
    own_mixed = staged_sum(forward_terms, COL, col_sizes).astype(jnp.bfloat16)
    own_sum = jnp.dot(own_mixed, weight, preferred_element_type=jnp.float32)
    output = jax.nn.silu(own_sum).astype(jnp.bfloat16)
    own_upstream = (cotangent.astype(jnp.float32) * silu_slope(own_sum)).astype(jnp.bfloat16)
    weight_term = lax.dot_general(
        own_mixed, own_upstream, (((0,), (0,)), ((), ())), preferred_element_type=jnp.float32
    )
    on_chip = weight_term.reshape(tuple(row_sizes) + (-1, weight_term.shape[1]))
    on_chip = jnp.moveaxis(on_chip, 2, 0)
    on_chip = lax.all_to_all(on_chip, ROW[2], 0, 0, tiled=False).sum(0)
    weight_part = exchange_sum(on_chip.reshape((-1, weight_term.shape[1])), ROW[:2], row_count // row_sizes[2])
    weight_part = exchange_sum(weight_part, COL, col_count)
    grad_weight = exchange_gather(exchange_gather(weight_part, COL, col_count), ROW, row_count)
    upstream = lax.all_gather(own_upstream, COL, axis=0, tiled=True)
    upstream, grad_weight = lax.optimization_barrier((upstream, grad_weight))
    backward_terms = block_terms(
        values, row_ids, reversed_blocks(col_ids, row_sizes, parts_per_device), live_count,
        upstream, col_span // block_side, True
    )
    grad_projected = staged_sum(backward_terms, ROW, row_sizes).astype(jnp.bfloat16)
    grad_features = lax.dot_general(
        grad_projected, weight, (((1,), (1,)), ((), ())), preferred_element_type=jnp.float32
    ).astype(jnp.bfloat16)
    return (output, grad_features, grad_weight)


def solution(mesh):
    row_parts = (2, 4, 2)
    col_parts = (4, 4)
    split = Mesh(mesh.devices.reshape(row_parts + col_parts), ROW + COL)
    placed = (
        P(COL + ROW, None),
        P(),
        P(ROW, COL, None, None, None),
        P(ROW, COL, None),
        P(ROW, COL, None),
        P(ROW, COL),
        P(ROW + COL, None),
    )
    return jax.shard_map(
        shards,
        mesh=split,
        in_specs=placed,
        out_specs=(P(ROW + COL, None), P(COL + ROW, None), P()),
        check_vma=False,
    )
```

```python
import functools
import jax
import jax.numpy as jnp
from jax import lax
from jax.experimental import pallas as pl
from jax.experimental.pallas import tpu as pltpu
from jax.sharding import Mesh, PartitionSpec as P

GROUP = 8


def block_kernel(source_ids, target_ids, live, values_ref, *refs, transpose):
    tile_refs, out_ref, acc_ref, seen_ref = refs[:-3], refs[-3], refs[-2], refs[-1]
    step = pl.program_id(0)
    group = len(tile_refs)
    block_count, block_side, _ = acc_ref.shape

    @pl.when(step == 0)
    def _():
        for block in range(block_count):
            seen_ref[block] = 0

    for slot, tile_ref in enumerate(tile_refs):
        entry = step * group + slot

        @pl.when(entry < live[0])
        def _():
            block = values_ref[slot]
            if transpose:
                term = lax.dot_general(block, tile_ref[...], (((0,), (0,)), ((), ())), preferred_element_type=jnp.float32)
            else:
                term = jnp.dot(block, tile_ref[...], preferred_element_type=jnp.float32)
            target = target_ids[entry]
            fresh = seen_ref[target] == 0

            @pl.when(fresh)
            def _():
                acc_ref[target] = term

            @pl.when(jnp.logical_not(fresh))
            def _():
                acc_ref[target] += term

            seen_ref[target] = 1

    @pl.when(step == pl.num_programs(0) - 1)
    def _():
        for block in range(block_count):
            rows = pl.ds(block * block_side, block_side)
            touched = seen_ref[block] != 0

            @pl.when(touched)
            def _():
                out_ref[rows, :] = acc_ref[block].astype(out_ref.dtype)

            @pl.when(jnp.logical_not(touched))
            def _():
                out_ref[rows, :] = jnp.zeros((block_side, out_ref.shape[1]), out_ref.dtype)


def block_terms(values, source_ids, target_ids, live_count, source, target_blocks, transpose):
    entry_total, block_side, _ = values.shape
    feature_count = source.shape[1]
    group = GROUP
    live = jnp.reshape(live_count, (1,)).astype(jnp.int32)

    def values_map(step, source_ids, target_ids, live):
        return (jnp.minimum(step, (live[0] - 1) // group), 0, 0)

    def tile_map_of(slot):
        def tile_map(step, source_ids, target_ids, live):
            return (source_ids[jnp.minimum(step * group + slot, live[0] - 1)], 0)
        return tile_map

    def out_map(step, source_ids, target_ids, live):
        return (0, 0)

    grid_spec = pltpu.PrefetchScalarGridSpec(
        num_scalar_prefetch=3,
        grid=(entry_total // group,),
        in_specs=[pl.BlockSpec((group, block_side, block_side), values_map)]
        + [pl.BlockSpec((block_side, feature_count), tile_map_of(slot)) for slot in range(group)],
        out_specs=pl.BlockSpec((target_blocks * block_side, feature_count), out_map),
        scratch_shapes=[
            pltpu.VMEM((target_blocks, block_side, feature_count), jnp.float32),
            pltpu.SMEM((target_blocks,), jnp.int32),
        ],
    )
    return pl.pallas_call(
        functools.partial(block_kernel, transpose=transpose),
        grid_spec=grid_spec,
        out_shape=jax.ShapeDtypeStruct((target_blocks * block_side, feature_count), jnp.bfloat16),
        compiler_params=pltpu.CompilerParams(dimension_semantics=("arbitrary",)),
    )(source_ids, target_ids, live, values, *([source] * group))


ROW = ("zl", "x", "core")
COL = ("zh", "y")


def exchange_sum(parts, axis_name, count):
    pieces = parts.reshape((count, -1) + parts.shape[1:])
    pieces = lax.all_to_all(pieces, axis_name, 0, 0, tiled=False)
    return pieces.astype(jnp.float32).sum(0)


def reversed_blocks(target_ids, sizes, blocks_per_part):
    part, half = target_ids // blocks_per_part, target_ids % blocks_per_part
    flipped, stride = 0, 1
    for size in reversed(sizes):
        flipped = flipped * size + part % size
        part = part // size
    return flipped * blocks_per_part + half


def staged_sum(parts, axes, sizes):
    pieces = parts.reshape(tuple(reversed(sizes)) + (-1,) + parts.shape[1:])
    for position, name in enumerate(reversed(axes)):
        pieces = lax.all_to_all(pieces, name, 0, 0, tiled=False)
        pieces = pieces.astype(jnp.float32).sum(0)
        if position < len(axes) - 1:
            pieces = pieces.astype(jnp.bfloat16)
    return pieces


def exchange_gather(part, axis_name, count):
    pieces = jnp.broadcast_to(part[None], (count,) + part.shape)
    pieces = lax.all_to_all(pieces, axis_name, 0, 0, tiled=False)
    return pieces.reshape((-1,) + part.shape[1:])


def silu_slope(summed):
    sigmoid_value = jax.nn.sigmoid(summed)
    return sigmoid_value * (1.0 + summed * (1.0 - sigmoid_value))


def shards(features, weight, entry_values, block_rows, block_cols, entry_counts, cotangent):
    values = entry_values[0, 0]
    row_ids = block_rows[0, 0]
    col_ids = block_cols[0, 0]
    live_count = entry_counts[0, 0]
    local_rows = features.shape[0]
    block_side = values.shape[1]
    row_sizes = [lax.axis_size(name) for name in ROW]
    col_sizes = [lax.axis_size(name) for name in COL]
    row_count = row_sizes[0] * row_sizes[1] * row_sizes[2]
    col_count = col_sizes[0] * col_sizes[1]
    row_span = col_count * local_rows
    col_span = row_count * local_rows
    panel = lax.all_gather(features, ROW, axis=0, tiled=True)
    parts_per_device = local_rows // block_side
    forward_terms = block_terms(
        values, col_ids, reversed_blocks(row_ids, col_sizes, parts_per_device), live_count,
        panel, row_span // block_side, False
    )
    own_mixed = staged_sum(forward_terms, COL, col_sizes).astype(jnp.bfloat16)
    own_sum = jnp.dot(own_mixed, weight, preferred_element_type=jnp.float32)
    output = jax.nn.silu(own_sum).astype(jnp.bfloat16)
    own_upstream = (cotangent.astype(jnp.float32) * silu_slope(own_sum)).astype(jnp.bfloat16)
    weight_term = lax.dot_general(
        own_mixed, own_upstream, (((0,), (0,)), ((), ())), preferred_element_type=jnp.float32
    )
    on_chip = weight_term.reshape(tuple(row_sizes) + (-1, weight_term.shape[1]))
    on_chip = jnp.moveaxis(on_chip, 2, 0)
    on_chip = lax.all_to_all(on_chip, ROW[2], 0, 0, tiled=False).sum(0)
    weight_part = exchange_sum(on_chip.reshape((-1, weight_term.shape[1])), ROW[:2], row_count // row_sizes[2])
    weight_part = exchange_sum(weight_part, COL, col_count)
    weight_rows = exchange_gather(weight_part, COL, col_count)
    chip_rows = exchange_gather(weight_rows, ROW[:2], row_count // row_sizes[2])
    both_cores = exchange_gather(chip_rows[None], ROW[2], row_sizes[2])
    both_cores = both_cores.reshape((row_sizes[2], row_sizes[0], row_sizes[1]) + weight_rows.shape)
    grad_weight = jnp.moveaxis(both_cores, 0, 2).reshape((-1, weight_rows.shape[1]))
    upstream = lax.all_gather(own_upstream, COL, axis=0, tiled=True)
    upstream, grad_weight = lax.optimization_barrier((upstream, grad_weight))
    backward_terms = block_terms(
        values, row_ids, reversed_blocks(col_ids, row_sizes, parts_per_device), live_count,
        upstream, col_span // block_side, True
    )
    grad_projected = staged_sum(backward_terms, ROW, row_sizes).astype(jnp.bfloat16)
    grad_features = lax.dot_general(
        grad_projected, weight, (((1,), (1,)), ((), ())), preferred_element_type=jnp.float32
    ).astype(jnp.bfloat16)
    return (output, grad_features, grad_weight)


def solution(mesh):
    row_parts = (2, 4, 2)
    col_parts = (4, 4)
    split = Mesh(mesh.devices.reshape(row_parts + col_parts), ROW + COL)
    placed = (
        P(COL + ROW, None),
        P(),
        P(ROW, COL, None, None, None),
        P(ROW, COL, None),
        P(ROW, COL, None),
        P(ROW, COL),
        P(ROW + COL, None),
    )
    return jax.shard_map(
        shards,
        mesh=split,
        in_specs=placed,
        out_specs=(P(ROW + COL, None), P(COL + ROW, None), P()),
        check_vma=False,
    )
```

```python
import functools
import jax
import jax.numpy as jnp
from jax import lax
from jax.experimental import pallas as pl
from jax.experimental.pallas import tpu as pltpu
from jax.sharding import Mesh, PartitionSpec as P

GROUP = 8


def block_kernel(source_ids, target_ids, live, values_ref, *refs, transpose):
    tile_refs, out_ref, acc_ref, seen_ref = refs[:-3], refs[-3], refs[-2], refs[-1]
    step = pl.program_id(0)
    group = len(tile_refs)
    block_count, block_side, _ = acc_ref.shape

    @pl.when(step == 0)
    def _():
        for block in range(block_count):
            seen_ref[block] = 0

    for slot, tile_ref in enumerate(tile_refs):
        entry = step * group + slot

        @pl.when(entry < live[0])
        def _():
            block = values_ref[slot]
            if transpose:
                term = lax.dot_general(block, tile_ref[...], (((0,), (0,)), ((), ())), preferred_element_type=jnp.float32)
            else:
                term = jnp.dot(block, tile_ref[...], preferred_element_type=jnp.float32)
            target = target_ids[entry]
            fresh = seen_ref[target] == 0

            @pl.when(fresh)
            def _():
                acc_ref[target] = term

            @pl.when(jnp.logical_not(fresh))
            def _():
                acc_ref[target] += term

            seen_ref[target] = 1

    @pl.when(step == pl.num_programs(0) - 1)
    def _():
        for block in range(block_count):
            rows = pl.ds(block * block_side, block_side)
            touched = seen_ref[block] != 0

            @pl.when(touched)
            def _():
                out_ref[rows, :] = acc_ref[block].astype(out_ref.dtype)

            @pl.when(jnp.logical_not(touched))
            def _():
                out_ref[rows, :] = jnp.zeros((block_side, out_ref.shape[1]), out_ref.dtype)


def block_terms(values, source_ids, target_ids, live_count, source, target_blocks, transpose):
    entry_total, block_side, _ = values.shape
    feature_count = source.shape[1]
    group = GROUP
    live = jnp.reshape(live_count, (1,)).astype(jnp.int32)

    def values_map(step, source_ids, target_ids, live):
        return (jnp.minimum(step, (live[0] - 1) // group), 0, 0)

    def tile_map_of(slot):
        def tile_map(step, source_ids, target_ids, live):
            return (source_ids[jnp.minimum(step * group + slot, live[0] - 1)], 0)
        return tile_map

    def out_map(step, source_ids, target_ids, live):
        return (0, 0)

    grid_spec = pltpu.PrefetchScalarGridSpec(
        num_scalar_prefetch=3,
        grid=(entry_total // group,),
        in_specs=[pl.BlockSpec((group, block_side, block_side), values_map)]
        + [pl.BlockSpec((block_side, feature_count), tile_map_of(slot)) for slot in range(group)],
        out_specs=pl.BlockSpec((target_blocks * block_side, feature_count), out_map),
        scratch_shapes=[
            pltpu.VMEM((target_blocks, block_side, feature_count), jnp.float32),
            pltpu.SMEM((target_blocks,), jnp.int32),
        ],
    )
    return pl.pallas_call(
        functools.partial(block_kernel, transpose=transpose),
        grid_spec=grid_spec,
        out_shape=jax.ShapeDtypeStruct((target_blocks * block_side, feature_count), jnp.bfloat16),
        compiler_params=pltpu.CompilerParams(dimension_semantics=("arbitrary",)),
    )(source_ids, target_ids, live, values, *([source] * group))


ROW = ("zl", "x", "core")
COL = ("zh", "y")


def exchange_sum(parts, axis_name, count):
    pieces = parts.reshape((count, -1) + parts.shape[1:])
    pieces = lax.all_to_all(pieces, axis_name, 0, 0, tiled=False)
    return pieces.astype(jnp.float32).sum(0)


def reversed_blocks(target_ids, sizes, blocks_per_part):
    part, half = target_ids // blocks_per_part, target_ids % blocks_per_part
    flipped, stride = 0, 1
    for size in reversed(sizes):
        flipped = flipped * size + part % size
        part = part // size
    return flipped * blocks_per_part + half


def staged_sum(parts, axes, sizes):
    pieces = parts.reshape(tuple(reversed(sizes)) + (-1,) + parts.shape[1:])
    for position, name in enumerate(reversed(axes)):
        pieces = lax.all_to_all(pieces, name, 0, 0, tiled=False)
        pieces = pieces.astype(jnp.float32).sum(0)
        if position < len(axes) - 1:
            pieces = pieces.astype(jnp.bfloat16)
    return pieces


def exchange_gather(part, axis_name, count):
    pieces = jnp.broadcast_to(part[None], (count,) + part.shape)
    pieces = lax.all_to_all(pieces, axis_name, 0, 0, tiled=False)
    return pieces.reshape((-1,) + part.shape[1:])


def silu_slope(summed):
    sigmoid_value = jax.nn.sigmoid(summed)
    return sigmoid_value * (1.0 + summed * (1.0 - sigmoid_value))


def shards(features, weight, entry_values, block_rows, block_cols, entry_counts, cotangent):
    values = entry_values[0, 0]
    row_ids = block_rows[0, 0]
    col_ids = block_cols[0, 0]
    live_count = entry_counts[0, 0]
    local_rows = features.shape[0]
    block_side = values.shape[1]
    row_sizes = [lax.axis_size(name) for name in ROW]
    col_sizes = [lax.axis_size(name) for name in COL]
    row_count = row_sizes[0] * row_sizes[1] * row_sizes[2]
    col_count = col_sizes[0] * col_sizes[1]
    row_span = col_count * local_rows
    col_span = row_count * local_rows
    panel = lax.all_gather(features, ROW, axis=0, tiled=True)
    parts_per_device = local_rows // block_side
    chip_sizes = [row_sizes[0] * row_sizes[1], row_sizes[2]]
    forward_terms = block_terms(
        values, col_ids, reversed_blocks(row_ids, col_sizes, parts_per_device), live_count,
        panel, row_span // block_side, False
    )
    own_mixed = staged_sum(forward_terms, COL, col_sizes).astype(jnp.bfloat16)
    own_sum = jnp.dot(own_mixed, weight, preferred_element_type=jnp.float32)
    output = jax.nn.silu(own_sum).astype(jnp.bfloat16)
    own_upstream = (cotangent.astype(jnp.float32) * silu_slope(own_sum)).astype(jnp.bfloat16)
    weight_term = lax.dot_general(
        own_mixed, own_upstream, (((0,), (0,)), ((), ())), preferred_element_type=jnp.float32
    )
    on_chip = weight_term.reshape(tuple(row_sizes) + (-1, weight_term.shape[1]))
    on_chip = jnp.moveaxis(on_chip, 2, 0)
    on_chip = lax.all_to_all(on_chip, ROW[2], 0, 0, tiled=False).sum(0)
    weight_part = exchange_sum(on_chip.reshape((-1, weight_term.shape[1])), ROW[:2], row_count // row_sizes[2])
    weight_part = exchange_sum(weight_part, COL, col_count)
    weight_rows = exchange_gather(weight_part, COL, col_count)
    chip_rows = exchange_gather(weight_rows, ROW[:2], row_count // row_sizes[2])
    both_cores = exchange_gather(chip_rows[None], ROW[2], row_sizes[2])
    both_cores = both_cores.reshape((row_sizes[2], row_sizes[0], row_sizes[1]) + weight_rows.shape)
    grad_weight = jnp.moveaxis(both_cores, 0, 2).reshape((-1, weight_rows.shape[1]))
    upstream = lax.all_gather(own_upstream, COL, axis=0, tiled=True)
    upstream, grad_weight = lax.optimization_barrier((upstream, grad_weight))
    backward_terms = block_terms(
        values, row_ids, reversed_blocks(col_ids, chip_sizes, parts_per_device), live_count,
        upstream, col_span // block_side, True
    )
    grad_projected = staged_sum(backward_terms, (ROW[:2], ROW[2]), chip_sizes).astype(jnp.bfloat16)
    grad_features = lax.dot_general(
        grad_projected, weight, (((1,), (1,)), ((), ())), preferred_element_type=jnp.float32
    ).astype(jnp.bfloat16)
    return (output, grad_features, grad_weight)


def solution(mesh):
    row_parts = (2, 4, 2)
    col_parts = (4, 4)
    split = Mesh(mesh.devices.reshape(row_parts + col_parts), ROW + COL)
    placed = (
        P(COL + ROW, None),
        P(),
        P(ROW, COL, None, None, None),
        P(ROW, COL, None),
        P(ROW, COL, None),
        P(ROW, COL),
        P(ROW + COL, None),
    )
    return jax.shard_map(
        shards,
        mesh=split,
        in_specs=placed,
        out_specs=(P(ROW + COL, None), P(COL + ROW, None), P()),
        check_vma=False,
    )
```
